256 devices in a mesh: row: 16 (over y, x), col: 16 (over z, core).
Axes of the slice: x: 4, y: 4, z: 8, core: 2. Of those that a mesh axis runs over, the one named last changes fastest.
Arguments:
- q_seq: bfloat16 [2048, 6144], P('row', 'col'), may hold values from -4.5 to 4.5
- k_seq: bfloat16 [2048, 6144], P('row', 'col'), may hold values from -4.5 to 4.5
- v_seq: bfloat16 [2048, 6144], P('row', 'col'), may hold values from -6 to 6
- resid: bfloat16 [2048, 6144], P('row', 'col'), may hold values from -90 to 90
- ln_gain: float32 [6144], replicated, may hold values from 0.1 to 1.9
- w_up: bfloat16 [6144, 24576], P('row', 'col'), may hold values from -0.078125 to 0.078125
Outputs:
- hidden: bfloat16 [2048, 24576], P('row', 'col')
The draws below stay inside these ranges and needn't reach their ends.
All inputs are finite; a program needn't handle non-finite values.
Results may differ from the reference program's by a relative error of at most 0.0051.
Values may be sent and summed in bfloat16 or wider, within the bound.
No kernel may reach another device: no remote copies, remote signals or barrier semaphores. Data moves between devices by JAX's collectives and lax.ppermute only.
A program may use at most 64 MiB of HBM per device.

```python
import math
import jax
import jax.numpy as jnp
from jax import lax

HD = 128
FF = 24576
SEQ = 128
D = 6144
TOKENS = 2048
N_ROW = 16


def draw_q_seq(key, part):
    values = jnp.clip(jax.random.normal(jax.random.fold_in(key, 1), (TOKENS, D), jnp.float32), -4.5, 4.5)
    return values.astype(jnp.bfloat16)


def draw_k_seq(key, part):
    values = jnp.clip(jax.random.normal(jax.random.fold_in(key, 2), (TOKENS, D), jnp.float32), -4.5, 4.5)
    return values.astype(jnp.bfloat16)


def draw_resid(key, part):
    first = jax.random.fold_in(key, 11)
    second = jax.random.fold_in(key, 12)
    third = jax.random.fold_in(key, 13)
    column = jnp.arange(D).astype(jnp.float32) / D
    base = jnp.clip(jax.random.normal(first, (TOKENS, D), jnp.float32), -4.0, 4.0)
    scales = jnp.exp(jnp.log(0.3) + jnp.log(10.0) * column)
    scales = scales * jax.random.uniform(second, (D,), jnp.float32, 0.7, 1.4)
    row_scale = 0.5 * jnp.exp(jax.random.uniform(third, (TOKENS, 1), jnp.float32) * jnp.log(10.0))
    return (base * scales[None, :] * row_scale).astype(jnp.bfloat16)


def block_scale(own_key, extent, split, least, high):
    level = 1.0
    for dim, blocks in split:
        draws = jax.random.uniform(jax.random.fold_in(jax.random.fold_in(own_key, 6), dim), (blocks,), jnp.float32, least / len(split), high / len(split))
        level = level * jnp.repeat(jnp.exp(draws), extent[dim] // blocks).reshape((-1,) + (1,) * (len(extent) - 1 - dim))
    return level


def scatter_about(rng, shape, scale, most, shards=(), kind=jnp.bfloat16):
    factor_of = block_scale(rng, shape, shards, -0.22, 0.18) if shards else 1.0
    entries = jax.random.normal(rng, shape, jnp.float32) * scale * factor_of
    return jnp.minimum(jnp.maximum(entries, -most), most).astype(kind)


def setup_inputs(seed: int = 0) -> dict:
    seeds = jax.random.split(jax.random.key(seed), 7)
    q_seq = draw_q_seq(jax.random.fold_in(seeds[6], 71), 0)
    k_seq = draw_k_seq(jax.random.fold_in(seeds[6], 71), 0)
    v_seq = scatter_about(seeds[2], (TOKENS, D), 1.0, 6.0, ((0, 16), (1, 16)))
    resid = draw_resid(jax.random.fold_in(seeds[6], 71), 0)
    ln_gain = jnp.clip(1.0 + 0.18 * jax.random.normal(seeds[4], (D,), jnp.float32), 0.1, 1.9)
    w_up = scatter_about(seeds[5], (D, FF), D ** -0.5, 0.078125, ((0, 16), (1, 16)))
    return dict(q_seq=q_seq, k_seq=k_seq, v_seq=v_seq, resid=resid, ln_gain=ln_gain, w_up=w_up)


def attention_block(query, keys, values):
    seq, width = query.shape
    heads = width // HD
    qfloat = query.reshape(seq, heads, HD).astype(jnp.float32)
    kfloat = keys.reshape(seq, heads, HD).astype(jnp.float32)
    vfloat = values.reshape(seq, heads, HD).astype(jnp.float32)
    scores = jnp.einsum('qhd,khd->hqk', qfloat, kfloat) * (1.0 / math.sqrt(HD))
    rows_idx = lax.broadcasted_iota(jnp.int32, (seq, seq), 0)
    cols_idx = lax.broadcasted_iota(jnp.int32, (seq, seq), 1)
    scores = jnp.where((rows_idx >= cols_idx)[None], scores, -1e+30)
    highest = lax.optimization_barrier(jnp.max(scores, axis=-1, keepdims=True))
    expo = jnp.exp(scores - highest)
    prob = (expo / lax.optimization_barrier(jnp.sum(expo, axis=-1, keepdims=True))).astype(jnp.bfloat16)
    output = jnp.einsum('hqk,khd->qhd', prob.astype(jnp.float32), vfloat)
    return output.astype(jnp.bfloat16).reshape(seq, width)

def normalize(stream, gain):
    width = stream.shape[1]
    mean = lax.optimization_barrier(jnp.sum(stream, axis=1, keepdims=True)) / width
    spread = lax.optimization_barrier(jnp.sum(stream * stream, axis=1, keepdims=True)) / width - mean * mean
    return ((stream - mean) * lax.rsqrt(spread + 1e-05) * gain[None, :]).astype(jnp.bfloat16)

def reference(q_seq, k_seq, v_seq, resid, ln_gain, w_up):
    shaped = (N_ROW, SEQ, D)

    def attend_blocks(blocks):
        return attention_block(blocks[0], blocks[1], blocks[2])
    attended = lax.map(attend_blocks, (q_seq.reshape(shaped), k_seq.reshape(shaped), v_seq.reshape(shaped)))

    def layer_rows(blocks):
        stream = blocks[0].astype(jnp.float32) + blocks[1].astype(jnp.float32)
        normed = normalize(stream, ln_gain)
        product = jnp.dot(normed, w_up, preferred_element_type=jnp.float32)
        return jax.nn.gelu(product, approximate=True).astype(jnp.bfloat16)
    hidden = lax.map(layer_rows, (resid.reshape(shaped), attended))
    return hidden.reshape(TOKENS, FF)
```

```python
import math

import jax
import jax.numpy as jnp
from jax import lax
from jax.sharding import Mesh, PartitionSpec as P

HD = 128


def attention_block(query, keys, values):
    seq, width = query.shape
    heads = width // HD
    qshaped = query.reshape(seq, heads, HD)
    kshaped = keys.reshape(seq, heads, HD)
    vshaped = values.reshape(seq, heads, HD)
    scores = jnp.einsum("qhd,khd->hqk", qshaped, kshaped, preferred_element_type=jnp.float32)
    scores = scores * (1.0 / math.sqrt(HD))
    rows_idx = lax.broadcasted_iota(jnp.int32, (seq, seq), 0)
    cols_idx = lax.broadcasted_iota(jnp.int32, (seq, seq), 1)
    scores = jnp.where((rows_idx >= cols_idx)[None], scores, -1e30)
    highest = jnp.max(scores, axis=-1, keepdims=True)
    expo = jnp.exp(scores - highest)
    prob = (expo / jnp.sum(expo, axis=-1, keepdims=True)).astype(jnp.bfloat16)
    output = jnp.einsum("hqk,khd->qhd", prob, vshaped, preferred_element_type=jnp.float32)
    return output.astype(jnp.bfloat16).reshape(seq, width)


def per_device(q_seq, k_seq, v_seq, resid, ln_gain, w_up, full_width):
    w_group = lax.all_gather(w_up, "rx", axis=0, tiled=True)
    attended = attention_block(q_seq, k_seq, v_seq)
    stream = resid.astype(jnp.float32) + attended.astype(jnp.float32)
    width = stream.shape[1]
    sums = jnp.concatenate(
        [jnp.sum(stream, axis=1, keepdims=True), jnp.sum(stream * stream, axis=1, keepdims=True)], axis=1
    )
    sums = lax.psum(sums, "col")
    mean = sums[:, 0:1] / full_width
    spread = sums[:, 1:2] / full_width - mean * mean
    col = lax.axis_index("col")
    gain = lax.dynamic_slice_in_dim(ln_gain, col * width, width)
    normed = ((stream - mean) * lax.rsqrt(spread + 1e-05) * gain[None, :]).astype(jnp.bfloat16)
    whole = lax.all_gather(normed, "col", axis=1, tiled=True)
    tokens = lax.all_to_all(whole, "ry", split_axis=1, concat_axis=0, tiled=True)
    partial = jnp.dot(tokens, w_group, preferred_element_type=jnp.float32)
    product = lax.psum_scatter(partial, "ry", scatter_dimension=0, tiled=True)
    return jax.nn.gelu(product, approximate=True).astype(jnp.bfloat16)


def solution(mesh):
    n_row, n_col = mesh.shape["row"], mesh.shape["col"]
    nx = len({d.coords[0] for d in mesh.devices[:, 0]})
    split = Mesh(mesh.devices.reshape(n_row // nx, nx, n_col), ("ry", "rx", "col"))
    rows = ("ry", "rx")
    placed = (
        P(rows, "col"),
        P(rows, "col"),
        P(rows, "col"),
        P(rows, "col"),
        P(),
        P(rows, "col"),
    )

    def body(q_seq, k_seq, v_seq, resid, ln_gain, w_up):
        return per_device(q_seq, k_seq, v_seq, resid, ln_gain, w_up, float(ln_gain.shape[0]))

    return jax.shard_map(body, mesh=split, in_specs=placed, out_specs=P(rows, "col"), check_vma=False)
```

```python
import math

import jax
import jax.numpy as jnp
from jax import lax
from jax.sharding import Mesh, PartitionSpec as P

HD = 128


def attention_block(query, keys, values):
    seq, width = query.shape
    heads = width // HD
    qshaped = query.reshape(seq, heads, HD)
    kshaped = keys.reshape(seq, heads, HD)
    vshaped = values.reshape(seq, heads, HD)
    scores = jnp.einsum("qhd,khd->hqk", qshaped, kshaped, preferred_element_type=jnp.float32)
    scores = scores * (1.0 / math.sqrt(HD))
    rows_idx = lax.broadcasted_iota(jnp.int32, (seq, seq), 0)
    cols_idx = lax.broadcasted_iota(jnp.int32, (seq, seq), 1)
    scores = jnp.where((rows_idx >= cols_idx)[None], scores, -1e30)
    highest = jnp.max(scores, axis=-1, keepdims=True)
    expo = jnp.exp(scores - highest)
    prob = (expo / jnp.sum(expo, axis=-1, keepdims=True)).astype(jnp.bfloat16)
    output = jnp.einsum("hqk,khd->qhd", prob, vshaped, preferred_element_type=jnp.float32)
    return output.astype(jnp.bfloat16).reshape(seq, width)


def per_device(q_seq, k_seq, v_seq, resid, ln_gain, w_up):
    w_group = lax.all_gather(w_up, "rx", axis=0, tiled=True)
    res_tokens = lax.all_to_all(resid, "col", split_axis=0, concat_axis=1, tiled=True)
    attended = attention_block(q_seq, k_seq, v_seq)
    att_tokens = lax.all_to_all(attended, "col", split_axis=0, concat_axis=1, tiled=True)
    stream = res_tokens.astype(jnp.float32) + att_tokens.astype(jnp.float32)
    full_width = stream.shape[1]
    mean = jnp.sum(stream, axis=1, keepdims=True) / full_width
    spread = jnp.sum(stream * stream, axis=1, keepdims=True) / full_width - mean * mean
    normed = ((stream - mean) * lax.rsqrt(spread + 1e-05) * ln_gain[None, :]).astype(jnp.bfloat16)
    part = lax.all_to_all(normed, "ry", split_axis=1, concat_axis=0, tiled=True)
    n_y = part.shape[0] // normed.shape[0]
    part = part.reshape(n_y, normed.shape[0], part.shape[1])
    tokens = lax.all_gather(part, "col", axis=0, tiled=False)
    partial = jnp.einsum("cytf,fu->yctu", tokens, w_group, preferred_element_type=jnp.float32)
    partial = partial.reshape(-1, partial.shape[-1])
    product = lax.psum_scatter(partial, "ry", scatter_dimension=0, tiled=True)
    return jax.nn.gelu(product, approximate=True).astype(jnp.bfloat16)


def solution(mesh):
    n_row, n_col = mesh.shape["row"], mesh.shape["col"]
    nx = len({d.coords[0] for d in mesh.devices[:, 0]})
    split = Mesh(mesh.devices.reshape(n_row // nx, nx, n_col), ("ry", "rx", "col"))
    rows = ("ry", "rx")
    placed = (
        P(rows, "col"),
        P(rows, "col"),
        P(rows, "col"),
        P(rows, "col"),
        P(),
        P(rows, "col"),
    )

    def body(q_seq, k_seq, v_seq, resid, ln_gain, w_up):
        return per_device(q_seq, k_seq, v_seq, resid, ln_gain, w_up)

    return jax.shard_map(body, mesh=split, in_specs=placed, out_specs=P(rows, "col"), check_vma=False)
```

```python
import math

import jax
import jax.numpy as jnp
from jax import lax
from jax.sharding import Mesh, PartitionSpec as P

HD = 128


def attention_block(query, keys, values):
    seq, width = query.shape
    heads = width // HD
    qshaped = query.reshape(seq, heads, HD)
    kshaped = keys.reshape(seq, heads, HD)
    vshaped = values.reshape(seq, heads, HD)
    scores = jnp.einsum("qhd,khd->hqk", qshaped, kshaped, preferred_element_type=jnp.float32)
    scores = scores * (1.0 / math.sqrt(HD))
    rows_idx = lax.broadcasted_iota(jnp.int32, (seq, seq), 0)
    cols_idx = lax.broadcasted_iota(jnp.int32, (seq, seq), 1)
    scores = jnp.where((rows_idx >= cols_idx)[None], scores, -1e30)
    highest = jnp.max(scores, axis=-1, keepdims=True)
    expo = jnp.exp(scores - highest)
    prob = (expo / jnp.sum(expo, axis=-1, keepdims=True)).astype(jnp.bfloat16)
    output = jnp.einsum("hqk,khd->qhd", prob, vshaped, preferred_element_type=jnp.float32)
    return output.astype(jnp.bfloat16).reshape(seq, width)


def gather_ring(block, axis, n):
    if n != 4:
        whole = lax.all_gather(block, axis, axis=0, tiled=False)
        me = lax.axis_index(axis)
        order = (me + jnp.arange(n)) % n
        return jnp.take(whole, order, axis=0).reshape((-1,) + block.shape[1:])
    to_right = [(i, (i + 1) % n) for i in range(n)]
    to_left = [(i, (i - 1) % n) for i in range(n)]
    from_left = lax.ppermute(block, axis, to_right)
    from_right = lax.ppermute(block, axis, to_left)
    half = block.shape[0] // 2
    far_low = lax.ppermute(from_left[:half], axis, to_right)
    far_high = lax.ppermute(from_right[half:], axis, to_left)
    return jnp.concatenate([block, from_right, far_low, far_high, from_left], axis=0)


def per_device(q_seq, k_seq, v_seq, resid, ln_gain, w_up, n_x):
    w_group = gather_ring(w_up, "rx", n_x)
    res_tokens = lax.all_to_all(resid, "col", split_axis=0, concat_axis=1, tiled=True)
    attended = attention_block(q_seq, k_seq, v_seq)
    att_tokens = lax.all_to_all(attended, "col", split_axis=0, concat_axis=1, tiled=True)
    stream = res_tokens.astype(jnp.float32) + att_tokens.astype(jnp.float32)
    full_width = stream.shape[1]
    mean = jnp.sum(stream, axis=1, keepdims=True) / full_width
    spread = jnp.sum(stream * stream, axis=1, keepdims=True) / full_width - mean * mean
    normed = ((stream - mean) * lax.rsqrt(spread + 1e-05) * ln_gain[None, :]).astype(jnp.bfloat16)
    part = lax.all_to_all(normed, "ry", split_axis=1, concat_axis=0, tiled=True)
    n_y = part.shape[0] // normed.shape[0]
    part = part.reshape(n_y, normed.shape[0], part.shape[1])
    tokens = lax.all_gather(part, "col", axis=0, tiled=False)
    block = w_up.shape[0]
    doubled = jnp.concatenate([tokens, tokens], axis=3)
    tokens = lax.dynamic_slice_in_dim(doubled, lax.axis_index("rx") * block, tokens.shape[3], axis=3)
    partial = jnp.einsum("cytf,fu->yctu", tokens, w_group, preferred_element_type=jnp.float32)
    partial = partial.reshape(-1, partial.shape[-1])
    product = lax.psum_scatter(partial, "ry", scatter_dimension=0, tiled=True)
    return jax.nn.gelu(product, approximate=True).astype(jnp.bfloat16)


def solution(mesh):
    n_row, n_col = mesh.shape["row"], mesh.shape["col"]
    nx = len({d.coords[0] for d in mesh.devices[:, 0]})
    split = Mesh(mesh.devices.reshape(n_row // nx, nx, n_col), ("ry", "rx", "col"))
    rows = ("ry", "rx")
    placed = (
        P(rows, "col"),
        P(rows, "col"),
        P(rows, "col"),
        P(rows, "col"),
        P(),
        P(rows, "col"),
    )

    def body(q_seq, k_seq, v_seq, resid, ln_gain, w_up):
        return per_device(q_seq, k_seq, v_seq, resid, ln_gain, w_up, nx)

    return jax.shard_map(body, mesh=split, in_specs=placed, out_specs=P(rows, "col"), check_vma=False)
```

```python
import math

import jax
import jax.numpy as jnp
from jax import lax
from jax.experimental import pallas as pl
from jax.sharding import Mesh, PartitionSpec as P

HD = 128


def attention_block(query, keys, values):
    seq, width = query.shape
    heads = width // HD
    qshaped = query.reshape(seq, heads, HD)
    kshaped = keys.reshape(seq, heads, HD)
    vshaped = values.reshape(seq, heads, HD)
    scores = jnp.einsum("qhd,khd->hqk", qshaped, kshaped, preferred_element_type=jnp.float32)
    scores = scores * (1.0 / math.sqrt(HD))
    rows_idx = lax.broadcasted_iota(jnp.int32, (seq, seq), 0)
    cols_idx = lax.broadcasted_iota(jnp.int32, (seq, seq), 1)
    scores = jnp.where((rows_idx >= cols_idx)[None], scores, -1e30)
    highest = jnp.max(scores, axis=-1, keepdims=True)
    expo = jnp.exp(scores - highest)
    prob = (expo / jnp.sum(expo, axis=-1, keepdims=True)).astype(jnp.bfloat16)
    output = jnp.einsum("hqk,khd->qhd", prob, vshaped, preferred_element_type=jnp.float32)
    return output.astype(jnp.bfloat16).reshape(seq, width)


def ring_pieces(block, axis):
    n = 4
    to_right = [(i, (i + 1) % n) for i in range(n)]
    to_left = [(i, (i - 1) % n) for i in range(n)]
    from_left = lax.ppermute(block, axis, to_right)
    from_right = lax.ppermute(block, axis, to_left)
    half = block.shape[1] // 2
    far_low = lax.ppermute(from_left[:, :half], axis, to_right)
    far_high = lax.ppermute(from_right[:, half:], axis, to_left)
    return block, from_right, far_low, far_high, from_left


def pieces_kernel(a_ref, w0_ref, w1_ref, w2lo_ref, w2hi_ref, w3_ref, o_ref):
    k = w0_ref.shape[0]
    half = w2lo_ref.shape[1]
    a = a_ref[...]
    base = jnp.dot(a[:, 0:k], w0_ref[...], preferred_element_type=jnp.float32)
    base = base + jnp.dot(a[:, k:2 * k], w1_ref[...], preferred_element_type=jnp.float32)
    base = base + jnp.dot(a[:, 3 * k:4 * k], w3_ref[...], preferred_element_type=jnp.float32)
    far = a[:, 2 * k:3 * k]
    o_ref[:, 0:half] = base[:, 0:half] + jnp.dot(far, w2lo_ref[...], preferred_element_type=jnp.float32)
    o_ref[:, half:] = base[:, half:] + jnp.dot(far, w2hi_ref[...], preferred_element_type=jnp.float32)


def dot_pieces(a, pieces, tile=128):
    m, kk = a.shape
    n = pieces[0].shape[1]
    full = lambda p: pl.BlockSpec(p.shape, lambda i: (0, 0))
    return pl.pallas_call(
        pieces_kernel,
        grid=(m // tile,),
        in_specs=[pl.BlockSpec((tile, kk), lambda i: (i, 0))] + [full(p) for p in pieces],
        out_specs=pl.BlockSpec((tile, n), lambda i: (i, 0)),
        out_shape=jax.ShapeDtypeStruct((m, n), jnp.float32),
        cost_estimate=pl.CostEstimate(
            flops=2 * m * kk * n, transcendentals=0, bytes_accessed=a.size * 2 + sum(p.size * 2 for p in pieces) + m * n * 4
        ),
    )(a, *pieces)


def per_device(q_seq, k_seq, v_seq, resid, ln_gain, w_up, n_x):
    pieces = ring_pieces(w_up, "rx")
    res_tokens = lax.all_to_all(resid, "col", split_axis=0, concat_axis=1, tiled=True)
    attended = attention_block(q_seq, k_seq, v_seq)
    att_tokens = lax.all_to_all(attended, "col", split_axis=0, concat_axis=1, tiled=True)
    stream = res_tokens.astype(jnp.float32) + att_tokens.astype(jnp.float32)
    full_width = stream.shape[1]
    mean = jnp.sum(stream, axis=1, keepdims=True) / full_width
    spread = jnp.sum(stream * stream, axis=1, keepdims=True) / full_width - mean * mean
    normed = ((stream - mean) * lax.rsqrt(spread + 1e-05) * ln_gain[None, :]).astype(jnp.bfloat16)
    chunk, block = normed.shape[0], w_up.shape[0]
    n_y = full_width // (n_x * block)
    grouped = normed.reshape(chunk, n_y, n_x, block)
    doubled = jnp.concatenate([grouped, grouped], axis=2)
    rolled = lax.dynamic_slice_in_dim(doubled, lax.axis_index("rx"), n_x, axis=2).reshape(chunk, full_width)
    part = lax.all_to_all(rolled, "ry", split_axis=1, concat_axis=0, tiled=True)
    part = part.reshape(n_y, chunk, part.shape[1])
    tokens = lax.all_gather(part, "col", axis=1, tiled=True)
    tokens = tokens.reshape(-1, tokens.shape[-1])
    partial = dot_pieces(tokens, pieces)
    product = lax.psum_scatter(partial, "ry", scatter_dimension=0, tiled=True)
    return jax.nn.gelu(product, approximate=True).astype(jnp.bfloat16)


def solution(mesh):
    n_row, n_col = mesh.shape["row"], mesh.shape["col"]
    nx = len({d.coords[0] for d in mesh.devices[:, 0]})
    split = Mesh(mesh.devices.reshape(n_row // nx, nx, n_col), ("ry", "rx", "col"))
    rows = ("ry", "rx")
    placed = (
        P(rows, "col"),
        P(rows, "col"),
        P(rows, "col"),
        P(rows, "col"),
        P(),
        P(rows, "col"),
    )

    def body(q_seq, k_seq, v_seq, resid, ln_gain, w_up):
        return per_device(q_seq, k_seq, v_seq, resid, ln_gain, w_up, nx)

    return jax.shard_map(body, mesh=split, in_specs=placed, out_specs=P(rows, "col"), check_vma=False)
```

```python
import math

import jax
import jax.numpy as jnp
from jax import lax
from jax.experimental import pallas as pl
from jax.sharding import Mesh, PartitionSpec as P

HD = 128


def attention_block(query, keys, values):
    seq, width = query.shape
    heads = width // HD
    qshaped = query.reshape(seq, heads, HD)
    kshaped = keys.reshape(seq, heads, HD)
    vshaped = values.reshape(seq, heads, HD)
    scores = jnp.einsum("qhd,khd->hqk", qshaped, kshaped, preferred_element_type=jnp.float32)
    scores = scores * (1.0 / math.sqrt(HD))
    rows_idx = lax.broadcasted_iota(jnp.int32, (seq, seq), 0)
    cols_idx = lax.broadcasted_iota(jnp.int32, (seq, seq), 1)
    scores = jnp.where((rows_idx >= cols_idx)[None], scores, -1e30)
    highest = jnp.max(scores, axis=-1, keepdims=True)
    expo = jnp.exp(scores - highest)
    prob = (expo / jnp.sum(expo, axis=-1, keepdims=True)).astype(jnp.bfloat16)
    output = jnp.einsum("hqk,khd->qhd", prob, vshaped, preferred_element_type=jnp.float32)
    return output.astype(jnp.bfloat16).reshape(seq, width)


def ring_first(block, axis, anchor):
    n = 4
    to_right = [(i, (i + 1) % n) for i in range(n)]
    to_left = [(i, (i - 1) % n) for i in range(n)]
    from_left = lax.ppermute(block, axis, to_right)
    from_right = lax.ppermute(block, axis, to_left)
    return lax.optimization_barrier((from_left, from_right, anchor))


def ring_second(block, from_left, from_right, axis):
    n = 4
    to_right = [(i, (i + 1) % n) for i in range(n)]
    to_left = [(i, (i - 1) % n) for i in range(n)]
    half = block.shape[1] // 2
    far_low = lax.ppermute(from_left[:, :half], axis, to_right)
    far_high = lax.ppermute(from_right[:, half:], axis, to_left)
    return block, from_right, far_low, far_high, from_left


def pieces_kernel(a_ref, w0_ref, w1_ref, w2lo_ref, w2hi_ref, w3_ref, o_ref):
    k = w0_ref.shape[0]
    half = w2lo_ref.shape[1]
    a = a_ref[...]
    base = jnp.dot(a[:, 0:k], w0_ref[...], preferred_element_type=jnp.float32)
    base = base + jnp.dot(a[:, k:2 * k], w1_ref[...], preferred_element_type=jnp.float32)
    base = base + jnp.dot(a[:, 3 * k:4 * k], w3_ref[...], preferred_element_type=jnp.float32)
    far = a[:, 2 * k:3 * k]
    o_ref[:, 0:half] = base[:, 0:half] + jnp.dot(far, w2lo_ref[...], preferred_element_type=jnp.float32)
    o_ref[:, half:] = base[:, half:] + jnp.dot(far, w2hi_ref[...], preferred_element_type=jnp.float32)


def dot_pieces(a, pieces, tile=128):
    m, kk = a.shape
    n = pieces[0].shape[1]
    full = lambda p: pl.BlockSpec(p.shape, lambda i: (0, 0))
    return pl.pallas_call(
        pieces_kernel,
        grid=(m // tile,),
        in_specs=[pl.BlockSpec((tile, kk), lambda i: (i, 0))] + [full(p) for p in pieces],
        out_specs=pl.BlockSpec((tile, n), lambda i: (i, 0)),
        out_shape=jax.ShapeDtypeStruct((m, n), jnp.float32),
        cost_estimate=pl.CostEstimate(
            flops=2 * m * kk * n, transcendentals=0, bytes_accessed=a.size * 2 + sum(p.size * 2 for p in pieces) + m * n * 4
        ),
    )(a, *pieces)


def per_device(q_seq, k_seq, v_seq, resid, ln_gain, w_up, n_x):
    res_tokens = lax.all_to_all(resid, "col", split_axis=0, concat_axis=1, tiled=True)
    attended = attention_block(q_seq, k_seq, v_seq)
    rows = w_up.shape[0] // 2
    left_a, right_a, attended = ring_first(w_up[:rows], "rx", attended)
    att_tokens = lax.all_to_all(attended, "col", split_axis=0, concat_axis=1, tiled=True)
    stream = res_tokens.astype(jnp.float32) + att_tokens.astype(jnp.float32)
    full_width = stream.shape[1]
    mean = jnp.sum(stream, axis=1, keepdims=True) / full_width
    spread = jnp.sum(stream * stream, axis=1, keepdims=True) / full_width - mean * mean
    normed = ((stream - mean) * lax.rsqrt(spread + 1e-05) * ln_gain[None, :]).astype(jnp.bfloat16)
    left_b, right_b, normed = ring_first(w_up[rows:], "rx", normed)
    from_left = jnp.concatenate([left_a, left_b], axis=0)
    from_right = jnp.concatenate([right_a, right_b], axis=0)
    pieces = ring_second(w_up, from_left, from_right, "rx")
    chunk, block = normed.shape[0], w_up.shape[0]
    n_y = full_width // (n_x * block)
    grouped = normed.reshape(chunk, n_y, n_x, block)
    doubled = jnp.concatenate([grouped, grouped], axis=2)
    rolled = lax.dynamic_slice_in_dim(doubled, lax.axis_index("rx"), n_x, axis=2).reshape(chunk, full_width)
    part = lax.all_to_all(rolled, "ry", split_axis=1, concat_axis=0, tiled=True)
    part = part.reshape(n_y, chunk, part.shape[1])
    tokens = lax.all_gather(part, "col", axis=1, tiled=True)
    tokens = tokens.reshape(-1, tokens.shape[-1])
    partial = dot_pieces(tokens, pieces)
    product = lax.psum_scatter(partial, "ry", scatter_dimension=0, tiled=True)
    return jax.nn.gelu(product, approximate=True).astype(jnp.bfloat16)


def solution(mesh):
    n_row, n_col = mesh.shape["row"], mesh.shape["col"]
    nx = len({d.coords[0] for d in mesh.devices[:, 0]})
    split = Mesh(mesh.devices.reshape(n_row // nx, nx, n_col), ("ry", "rx", "col"))
    rows = ("ry", "rx")
    placed = (
        P(rows, "col"),
        P(rows, "col"),
        P(rows, "col"),
        P(rows, "col"),
        P(),
        P(rows, "col"),
    )

    def body(q_seq, k_seq, v_seq, resid, ln_gain, w_up):
        return per_device(q_seq, k_seq, v_seq, resid, ln_gain, w_up, nx)

    return jax.shard_map(body, mesh=split, in_specs=placed, out_specs=P(rows, "col"), check_vma=False)
```

```python
import math

import jax
import jax.numpy as jnp
from jax import lax
from jax.experimental import pallas as pl
from jax.sharding import Mesh, PartitionSpec as P

HD = 128


def attention_block(query, keys, values):
    seq, width = query.shape
    heads = width // HD
    qshaped = query.reshape(seq, heads, HD)
    kshaped = keys.reshape(seq, heads, HD)
    vshaped = values.reshape(seq, heads, HD)
    scores = jnp.einsum("qhd,khd->hqk", qshaped, kshaped, preferred_element_type=jnp.float32)
    scores = scores * (1.0 / math.sqrt(HD))
    rows_idx = lax.broadcasted_iota(jnp.int32, (seq, seq), 0)
    cols_idx = lax.broadcasted_iota(jnp.int32, (seq, seq), 1)
    scores = jnp.where((rows_idx >= cols_idx)[None], scores, -1e30)
    highest = jnp.max(scores, axis=-1, keepdims=True)
    expo = jnp.exp(scores - highest)
    prob = (expo / jnp.sum(expo, axis=-1, keepdims=True)).astype(jnp.bfloat16)
    output = jnp.einsum("hqk,khd->qhd", prob, vshaped, preferred_element_type=jnp.float32)
    return output.astype(jnp.bfloat16).reshape(seq, width)


def ring_pieces(block, axis):
    n = 4
    to_right = [(i, (i + 1) % n) for i in range(n)]
    to_left = [(i, (i - 1) % n) for i in range(n)]
    from_left = lax.ppermute(block, axis, to_right)
    from_right = lax.ppermute(block, axis, to_left)
    half = block.shape[1] // 2
    far_low = lax.ppermute(from_left[:, :half], axis, to_right)
    far_high = lax.ppermute(from_right[:, half:], axis, to_left)
    return block, from_right, far_low, far_high, from_left


def pieces_kernel(a_ref, w0_ref, w1_ref, w2lo_ref, w2hi_ref, w3_ref, o_ref):
    k = w0_ref.shape[0]
    half = w2lo_ref.shape[1]
    a = a_ref[...]
    base = jnp.dot(a[:, 0:k], w0_ref[...], preferred_element_type=jnp.float32)
    base = base + jnp.dot(a[:, k:2 * k], w1_ref[...], preferred_element_type=jnp.float32)
    base = base + jnp.dot(a[:, 3 * k:4 * k], w3_ref[...], preferred_element_type=jnp.float32)
    far = a[:, 2 * k:3 * k]
    o_ref[:, 0:half] = base[:, 0:half] + jnp.dot(far, w2lo_ref[...], preferred_element_type=jnp.float32)
    o_ref[:, half:] = base[:, half:] + jnp.dot(far, w2hi_ref[...], preferred_element_type=jnp.float32)


def dot_pieces(a, pieces, tile=128):
    m, kk = a.shape
    n = pieces[0].shape[1]
    full = lambda p: pl.BlockSpec(p.shape, lambda i: (0, 0))
    return pl.pallas_call(
        pieces_kernel,
        grid=(m // tile,),
        in_specs=[pl.BlockSpec((tile, kk), lambda i: (i, 0))] + [full(p) for p in pieces],
        out_specs=pl.BlockSpec((tile, n), lambda i: (i, 0)),
        out_shape=jax.ShapeDtypeStruct((m, n), jnp.float32),
        cost_estimate=pl.CostEstimate(
            flops=2 * m * kk * n, transcendentals=0, bytes_accessed=a.size * 2 + sum(p.size * 2 for p in pieces) + m * n * 4
        ),
    )(a, *pieces)


def per_device(q_seq, k_seq, v_seq, resid, ln_gain, w_up, n_x):
    pieces = ring_pieces(w_up, "rx")
    attended = attention_block(q_seq, k_seq, v_seq)
    both = jnp.stack([resid, attended], axis=1)
    both = lax.all_to_all(both, "col", split_axis=0, concat_axis=1, tiled=True)
    chunk = both.shape[0]
    both = both.reshape(chunk, -1, 2, resid.shape[1])
    stream = (both[:, :, 0].astype(jnp.float32) + both[:, :, 1].astype(jnp.float32)).reshape(chunk, -1)
    full_width = stream.shape[1]
    mean = jnp.sum(stream, axis=1, keepdims=True) / full_width
    spread = jnp.sum(stream * stream, axis=1, keepdims=True) / full_width - mean * mean
    normed = ((stream - mean) * lax.rsqrt(spread + 1e-05) * ln_gain[None, :]).astype(jnp.bfloat16)
    block = w_up.shape[0]
    n_y = full_width // (n_x * block)
    grouped = normed.reshape(chunk, n_y, n_x, block)
    doubled = jnp.concatenate([grouped, grouped], axis=2)
    rolled = lax.dynamic_slice_in_dim(doubled, lax.axis_index("rx"), n_x, axis=2).reshape(chunk, full_width)
    part = lax.all_to_all(rolled, "ry", split_axis=1, concat_axis=0, tiled=True)
    part = part.reshape(n_y, chunk, part.shape[1])
    tokens = lax.all_gather(part, "col", axis=1, tiled=True)
    tokens = tokens.reshape(-1, tokens.shape[-1])
    partial = dot_pieces(tokens, pieces)
    product = lax.psum_scatter(partial, "ry", scatter_dimension=0, tiled=True)
    return jax.nn.gelu(product, approximate=True).astype(jnp.bfloat16)


def solution(mesh):
    n_row, n_col = mesh.shape["row"], mesh.shape["col"]
    nx = len({d.coords[0] for d in mesh.devices[:, 0]})
    split = Mesh(mesh.devices.reshape(n_row // nx, nx, n_col), ("ry", "rx", "col"))
    rows = ("ry", "rx")
    placed = (
        P(rows, "col"),
        P(rows, "col"),
        P(rows, "col"),
        P(rows, "col"),
        P(),
        P(rows, "col"),
    )

    def body(q_seq, k_seq, v_seq, resid, ln_gain, w_up):
        return per_device(q_seq, k_seq, v_seq, resid, ln_gain, w_up, nx)

    return jax.shard_map(body, mesh=split, in_specs=placed, out_specs=P(rows, "col"), check_vma=False)
```

```python
import math

import jax
import jax.numpy as jnp
from jax import lax
from jax.experimental import pallas as pl
from jax.sharding import Mesh, PartitionSpec as P

HD = 128


def attention_block(query, keys, values):
    seq, width = query.shape
    heads = width // HD
    qshaped = query.reshape(seq, heads, HD)
    kshaped = keys.reshape(seq, heads, HD)
    vshaped = values.reshape(seq, heads, HD)
    scores = jnp.einsum("qhd,khd->hqk", qshaped, kshaped, preferred_element_type=jnp.float32)
    scores = scores * (1.0 / math.sqrt(HD))
    rows_idx = lax.broadcasted_iota(jnp.int32, (seq, seq), 0)
    cols_idx = lax.broadcasted_iota(jnp.int32, (seq, seq), 1)
    scores = jnp.where((rows_idx >= cols_idx)[None], scores, -1e30)
    highest = jnp.max(scores, axis=-1, keepdims=True)
    expo = jnp.exp(scores - highest)
    prob = (expo / jnp.sum(expo, axis=-1, keepdims=True)).astype(jnp.bfloat16)
    output = jnp.einsum("hqk,khd->qhd", prob, vshaped, preferred_element_type=jnp.float32)
    return output.astype(jnp.bfloat16).reshape(seq, width)


def ring_neighbours(block, axis):
    n = 4
    to_right = [(i, (i + 1) % n) for i in range(n)]
    to_left = [(i, (i - 1) % n) for i in range(n)]
    from_left = lax.ppermute(block, axis, to_right)
    from_right = lax.ppermute(block, axis, to_left)
    return from_left, from_right


def pieces_kernel(a_ref, w0_ref, w1_ref, w2_ref, w3_ref, o_ref):
    k = w0_ref.shape[0]
    a = a_ref[...]
    acc = jnp.dot(a[:, 0:k], w0_ref[...], preferred_element_type=jnp.float32)
    acc = acc + jnp.dot(a[:, k:2 * k], w1_ref[...], preferred_element_type=jnp.float32)
    acc = acc + jnp.dot(a[:, 2 * k:3 * k], w2_ref[...], preferred_element_type=jnp.float32)
    acc = acc + jnp.dot(a[:, 3 * k:4 * k], w3_ref[...], preferred_element_type=jnp.float32)
    o_ref[...] = acc


def dot_pieces(a, pieces, tile=128):
    m, kk = a.shape
    n = pieces[0].shape[1]
    full = lambda p: pl.BlockSpec(p.shape, lambda i: (0, 0))
    return pl.pallas_call(
        pieces_kernel,
        grid=(m // tile,),
        in_specs=[pl.BlockSpec((tile, kk), lambda i: (i, 0))] + [full(p) for p in pieces],
        out_specs=pl.BlockSpec((tile, n), lambda i: (i, 0)),
        out_shape=jax.ShapeDtypeStruct((m, n), jnp.float32),
        cost_estimate=pl.CostEstimate(
            flops=2 * m * kk * n, transcendentals=0, bytes_accessed=a.size * 2 + sum(p.size * 2 for p in pieces) + m * n * 4
        ),
    )(a, *pieces)


def per_device(q_seq, k_seq, v_seq, resid, ln_gain, w_up, n_x):
    pair = lax.all_gather(w_up, "rxh", axis=0, tiled=False)
    far = lax.dynamic_index_in_dim(pair, 1 - lax.axis_index("rxh"), 0, keepdims=False)
    from_left, from_right = ring_neighbours(w_up, ("rxh", "rxl"))
    pieces = (w_up, from_right, far, from_left)
    x_index = lax.axis_index("rxh") * 2 + lax.axis_index("rxl")
    attended = attention_block(q_seq, k_seq, v_seq)
    both = jnp.stack([resid, attended], axis=1)
    both = lax.all_to_all(both, "col", split_axis=0, concat_axis=1, tiled=True)
    chunk = both.shape[0]
    both = both.reshape(chunk, -1, 2, resid.shape[1])
    stream = (both[:, :, 0].astype(jnp.float32) + both[:, :, 1].astype(jnp.float32)).reshape(chunk, -1)
    full_width = stream.shape[1]
    mean = jnp.sum(stream, axis=1, keepdims=True) / full_width
    spread = jnp.sum(stream * stream, axis=1, keepdims=True) / full_width - mean * mean
    normed = ((stream - mean) * lax.rsqrt(spread + 1e-05) * ln_gain[None, :]).astype(jnp.bfloat16)
    block = w_up.shape[0]
    n_y = full_width // (n_x * block)
    grouped = normed.reshape(chunk, n_y, n_x, block)
    doubled = jnp.concatenate([grouped, grouped], axis=2)
    rolled = lax.dynamic_slice_in_dim(doubled, x_index, n_x, axis=2).reshape(chunk, full_width)
    part = lax.all_to_all(rolled, "ry", split_axis=1, concat_axis=0, tiled=True)
    part = part.reshape(n_y, chunk, part.shape[1])
    far, part = lax.optimization_barrier((far, part))
    pieces = (w_up, from_right, far, from_left)
    tokens = lax.all_gather(part, "col", axis=1, tiled=True)
    tokens = tokens.reshape(-1, tokens.shape[-1])
    partial = dot_pieces(tokens, pieces)
    product = lax.psum_scatter(partial, "ry", scatter_dimension=0, tiled=True)
    return jax.nn.gelu(product, approximate=True).astype(jnp.bfloat16)


def solution(mesh):
    n_row, n_col = mesh.shape["row"], mesh.shape["col"]
    nx = len({d.coords[0] for d in mesh.devices[:, 0]})
    assert nx == 4
    split = Mesh(mesh.devices.reshape(n_row // nx, 2, nx // 2, n_col), ("ry", "rxh", "rxl", "col"))
    rows = ("ry", "rxh", "rxl")
    placed = (
        P(rows, "col"),
        P(rows, "col"),
        P(rows, "col"),
        P(rows, "col"),
        P(),
        P(rows, "col"),
    )

    def body(q_seq, k_seq, v_seq, resid, ln_gain, w_up):
        return per_device(q_seq, k_seq, v_seq, resid, ln_gain, w_up, nx)

    return jax.shard_map(body, mesh=split, in_specs=placed, out_specs=P(rows, "col"), check_vma=False)
```

```python
import math

import jax
import jax.numpy as jnp
from jax import lax
from jax.experimental import pallas as pl
from jax.sharding import Mesh, PartitionSpec as P

HD = 128


def attention_block(query, keys, values):
    seq, width = query.shape
    heads = width // HD
    qshaped = query.reshape(seq, heads, HD)
    kshaped = keys.reshape(seq, heads, HD)
    vshaped = values.reshape(seq, heads, HD)
    scores = jnp.einsum("qhd,khd->hqk", qshaped, kshaped, preferred_element_type=jnp.float32)
    scores = scores * (1.0 / math.sqrt(HD))
    rows_idx = lax.broadcasted_iota(jnp.int32, (seq, seq), 0)
    cols_idx = lax.broadcasted_iota(jnp.int32, (seq, seq), 1)
    scores = jnp.where((rows_idx >= cols_idx)[None], scores, -1e30)
    highest = jnp.max(scores, axis=-1, keepdims=True)
    expo = jnp.exp(scores - highest)
    prob = (expo / jnp.sum(expo, axis=-1, keepdims=True)).astype(jnp.bfloat16)
    output = jnp.einsum("hqk,khd->qhd", prob, vshaped, preferred_element_type=jnp.float32)
    return output.astype(jnp.bfloat16).reshape(seq, width)


def ring_pieces(block, axis):
    n = 4
    to_right = [(i, (i + 1) % n) for i in range(n)]
    to_left = [(i, (i - 1) % n) for i in range(n)]
    width = block.shape[1] // 2
    near, far = [], []
    lefts, rights = [], []
    for c in range(2):
        piece = block[:, c * width:(c + 1) * width]
        lefts.append(lax.ppermute(piece, axis, to_right))
        rights.append(lax.ppermute(piece, axis, to_left))
    half = width // 2
    for c in range(2):
        far.append(lax.ppermute(lefts[c][:, :half], axis, to_right))
        far.append(lax.ppermute(rights[c][:, half:], axis, to_left))
    return (block, rights[0], rights[1], lefts[0], lefts[1]), tuple(far)


def near_kernel(a_ref, w0_ref, r0_ref, r1_ref, l0_ref, l1_ref, o_ref):
    k = w0_ref.shape[0]
    width = r0_ref.shape[1]
    a = a_ref[...]
    base = jnp.dot(a[:, 0:k], w0_ref[...], preferred_element_type=jnp.float32)
    own_right = a[:, k:2 * k]
    own_left = a[:, 3 * k:4 * k]
    for c, (r_ref, l_ref) in enumerate(((r0_ref, l0_ref), (r1_ref, l1_ref))):
        cols = slice(c * width, (c + 1) * width)
        side = jnp.dot(own_right, r_ref[...], preferred_element_type=jnp.float32)
        side = side + jnp.dot(own_left, l_ref[...], preferred_element_type=jnp.float32)
        o_ref[:, cols] = base[:, cols] + side


def far_kernel(a_ref, f0_ref, f1_ref, f2_ref, f3_ref, acc_ref, o_ref):
    k = a_ref.shape[1] // 4
    width = f0_ref.shape[1]
    far = a_ref[:, 2 * k:3 * k]
    for c, f_ref in enumerate((f0_ref, f1_ref, f2_ref, f3_ref)):
        cols = slice(c * width, (c + 1) * width)
        o_ref[:, cols] = acc_ref[:, cols] + jnp.dot(far, f_ref[...], preferred_element_type=jnp.float32)


def tiled_call(kernel, a, pieces, extra=(), tile=128):
    m, kk = a.shape
    n = 4 * pieces[0].shape[1] if kernel is far_kernel else pieces[0].shape[1]
    full = lambda p: pl.BlockSpec(p.shape, lambda i: (0, 0))
    rows = lambda width: pl.BlockSpec((tile, width), lambda i: (i, 0))
    flops = 2 * m * sum(p.shape[0] * p.shape[1] for p in pieces)
    moved = a.size * 2 + sum(p.size * 2 for p in pieces) + m * n * 4 * (1 + len(extra))
    return pl.pallas_call(
        kernel,
        grid=(m // tile,),
        in_specs=[rows(kk)] + [full(p) for p in pieces] + [rows(n) for _ in extra],
        out_specs=rows(n),
        out_shape=jax.ShapeDtypeStruct((m, n), jnp.float32),
        input_output_aliases={1 + len(pieces): 0} if extra else {},
        cost_estimate=pl.CostEstimate(flops=flops, transcendentals=0, bytes_accessed=moved),
    )(a, *pieces, *extra)


def per_device(q_seq, k_seq, v_seq, resid, ln_gain, w_up, n_x):
    pieces = ring_pieces(w_up, "rx")
    attended = attention_block(q_seq, k_seq, v_seq)
    both = jnp.stack([resid, attended], axis=1)
    both = lax.all_to_all(both, "col", split_axis=0, concat_axis=1, tiled=True)
    chunk = both.shape[0]
    both = both.reshape(chunk, -1, 2, resid.shape[1])
    stream = (both[:, :, 0].astype(jnp.float32) + both[:, :, 1].astype(jnp.float32)).reshape(chunk, -1)
    full_width = stream.shape[1]
    mean = jnp.sum(stream, axis=1, keepdims=True) / full_width
    spread = jnp.sum(stream * stream, axis=1, keepdims=True) / full_width - mean * mean
    normed = ((stream - mean) * lax.rsqrt(spread + 1e-05) * ln_gain[None, :]).astype(jnp.bfloat16)
    block = w_up.shape[0]
    n_y = full_width // (n_x * block)
    grouped = normed.reshape(chunk, n_y, n_x, block)
    doubled = jnp.concatenate([grouped, grouped], axis=2)
    rolled = lax.dynamic_slice_in_dim(doubled, lax.axis_index("rx"), n_x, axis=2).reshape(chunk, full_width)
    part = lax.all_to_all(rolled, "ry", split_axis=1, concat_axis=0, tiled=True)
    part = part.reshape(n_y, chunk, part.shape[1])
    tokens = lax.all_gather(part, "col", axis=1, tiled=True)
    tokens = tokens.reshape(-1, tokens.shape[-1])
    near, far = pieces
    partial = tiled_call(near_kernel, tokens, near)
    partial = tiled_call(far_kernel, tokens, far, extra=(partial,))
    product = lax.psum_scatter(partial, "ry", scatter_dimension=0, tiled=True)
    return jax.nn.gelu(product, approximate=True).astype(jnp.bfloat16)


def solution(mesh):
    n_row, n_col = mesh.shape["row"], mesh.shape["col"]
    nx = len({d.coords[0] for d in mesh.devices[:, 0]})
    split = Mesh(mesh.devices.reshape(n_row // nx, nx, n_col), ("ry", "rx", "col"))
    rows = ("ry", "rx")
    placed = (
        P(rows, "col"),
        P(rows, "col"),
        P(rows, "col"),
        P(rows, "col"),
        P(),
        P(rows, "col"),
    )

    def body(q_seq, k_seq, v_seq, resid, ln_gain, w_up):
        return per_device(q_seq, k_seq, v_seq, resid, ln_gain, w_up, nx)

    return jax.shard_map(body, mesh=split, in_specs=placed, out_specs=P(rows, "col"), check_vma=False)
```

```python
import math

import jax
import jax.numpy as jnp
from jax import lax
from jax.experimental import pallas as pl
from jax.sharding import Mesh, PartitionSpec as P

HD = 128


def attention_block(query, keys, values):
    seq, width = query.shape
    heads = width // HD
    qshaped = query.reshape(seq, heads, HD)
    kshaped = keys.reshape(seq, heads, HD)
    vshaped = values.reshape(seq, heads, HD)
    scores = jnp.einsum("qhd,khd->hqk", qshaped, kshaped, preferred_element_type=jnp.float32)
    scores = scores * (1.0 / math.sqrt(HD))
    rows_idx = lax.broadcasted_iota(jnp.int32, (seq, seq), 0)
    cols_idx = lax.broadcasted_iota(jnp.int32, (seq, seq), 1)
    scores = jnp.where((rows_idx >= cols_idx)[None], scores, -1e30)
    highest = jnp.max(scores, axis=-1, keepdims=True)
    expo = jnp.exp(scores - highest)
    prob = (expo / jnp.sum(expo, axis=-1, keepdims=True)).astype(jnp.bfloat16)
    output = jnp.einsum("hqk,khd->qhd", prob, vshaped, preferred_element_type=jnp.float32)
    return output.astype(jnp.bfloat16).reshape(seq, width)


def ring_near(block, axis, chunk, anchor):
    n = 4
    width = block.shape[1] // 2
    piece = block[:, chunk * width:(chunk + 1) * width]
    from_left = lax.ppermute(piece, axis, [(i, (i + 1) % n) for i in range(n)])
    from_right = lax.ppermute(piece, axis, [(i, (i - 1) % n) for i in range(n)])
    return lax.optimization_barrier((from_left, from_right, anchor))


def ring_far(lefts, rights, axis):
    n = 4
    half = lefts[0].shape[1] // 2
    far = []
    for from_left, from_right in zip(lefts, rights):
        far.append(lax.ppermute(from_left[:, :half], axis, [(i, (i + 1) % n) for i in range(n)]))
        far.append(lax.ppermute(from_right[:, half:], axis, [(i, (i - 1) % n) for i in range(n)]))
    return tuple(far)


def near_kernel(a_ref, w0_ref, r0_ref, r1_ref, l0_ref, l1_ref, o_ref):
    k = w0_ref.shape[0]
    width = r0_ref.shape[1]
    a = a_ref[...]
    base = jnp.dot(a[:, 0:k], w0_ref[...], preferred_element_type=jnp.float32)
    own_right = a[:, k:2 * k]
    own_left = a[:, 3 * k:4 * k]
    for c, (r_ref, l_ref) in enumerate(((r0_ref, l0_ref), (r1_ref, l1_ref))):
        cols = slice(c * width, (c + 1) * width)
        side = jnp.dot(own_right, r_ref[...], preferred_element_type=jnp.float32)
        side = side + jnp.dot(own_left, l_ref[...], preferred_element_type=jnp.float32)
        o_ref[:, cols] = base[:, cols] + side


def far_kernel(a_ref, f0_ref, f1_ref, f2_ref, f3_ref, acc_ref, o_ref):
    k = a_ref.shape[1] // 4
    width = f0_ref.shape[1]
    far = a_ref[:, 2 * k:3 * k]
    for c, f_ref in enumerate((f0_ref, f1_ref, f2_ref, f3_ref)):
        cols = slice(c * width, (c + 1) * width)
        o_ref[:, cols] = acc_ref[:, cols] + jnp.dot(far, f_ref[...], preferred_element_type=jnp.float32)


def tiled_call(kernel, a, pieces, extra=(), tile=128):
    m, kk = a.shape
    n = 4 * pieces[0].shape[1] if kernel is far_kernel else pieces[0].shape[1]
    full = lambda p: pl.BlockSpec(p.shape, lambda i: (0, 0))
    rows = lambda width: pl.BlockSpec((tile, width), lambda i: (i, 0))
    flops = 2 * m * sum(p.shape[0] * p.shape[1] for p in pieces)
    moved = a.size * 2 + sum(p.size * 2 for p in pieces) + m * n * 4 * (1 + len(extra))
    return pl.pallas_call(
        kernel,
        grid=(m // tile,),
        in_specs=[rows(kk)] + [full(p) for p in pieces] + [rows(n) for _ in extra],
        out_specs=rows(n),
        out_shape=jax.ShapeDtypeStruct((m, n), jnp.float32),
        input_output_aliases={1 + len(pieces): 0} if extra else {},
        cost_estimate=pl.CostEstimate(flops=flops, transcendentals=0, bytes_accessed=moved),
    )(a, *pieces, *extra)


def per_device(q_seq, k_seq, v_seq, resid, ln_gain, w_up, n_x):
    attended = attention_block(q_seq, k_seq, v_seq)
    both = jnp.stack([resid, attended], axis=1)
    both = lax.all_to_all(both, "col", split_axis=0, concat_axis=1, tiled=True)
    chunk = both.shape[0]
    both = both.reshape(chunk, -1, 2, resid.shape[1])
    stream = (both[:, :, 0].astype(jnp.float32) + both[:, :, 1].astype(jnp.float32)).reshape(chunk, -1)
    full_width = stream.shape[1]
    mean = jnp.sum(stream, axis=1, keepdims=True) / full_width
    spread = jnp.sum(stream * stream, axis=1, keepdims=True) / full_width - mean * mean
    normed = ((stream - mean) * lax.rsqrt(spread + 1e-05) * ln_gain[None, :]).astype(jnp.bfloat16)
    block = w_up.shape[0]
    n_y = full_width // (n_x * block)
    grouped = normed.reshape(chunk, n_y, n_x, block)
    doubled = jnp.concatenate([grouped, grouped], axis=2)
    rolled = lax.dynamic_slice_in_dim(doubled, lax.axis_index("rx"), n_x, axis=2).reshape(chunk, full_width)
    part = lax.all_to_all(rolled, "ry", split_axis=1, concat_axis=0, tiled=True)
    part = part.reshape(n_y, chunk, part.shape[1])
    left0, right0, part = ring_near(w_up, "rx", 0, part)
    left1, right1, part = ring_near(w_up, "rx", 1, part)
    far = ring_far((left0, left1), (right0, right1), "rx")
    near = (w_up, right0, right1, left0, left1)
    tokens = lax.all_gather(part, "col", axis=1, tiled=True)
    tokens = tokens.reshape(-1, tokens.shape[-1])
    partial = tiled_call(near_kernel, tokens, near)
    partial = tiled_call(far_kernel, tokens, far, extra=(partial,))
    product = lax.psum_scatter(partial, "ry", scatter_dimension=0, tiled=True)
    return jax.nn.gelu(product, approximate=True).astype(jnp.bfloat16)


def solution(mesh):
    n_row, n_col = mesh.shape["row"], mesh.shape["col"]
    nx = len({d.coords[0] for d in mesh.devices[:, 0]})
    split = Mesh(mesh.devices.reshape(n_row // nx, nx, n_col), ("ry", "rx", "col"))
    rows = ("ry", "rx")
    placed = (
        P(rows, "col"),
        P(rows, "col"),
        P(rows, "col"),
        P(rows, "col"),
        P(),
        P(rows, "col"),
    )

    def body(q_seq, k_seq, v_seq, resid, ln_gain, w_up):
        return per_device(q_seq, k_seq, v_seq, resid, ln_gain, w_up, nx)

    return jax.shard_map(body, mesh=split, in_specs=placed, out_specs=P(rows, "col"), check_vma=False)
```

```python
import math

import jax
import jax.numpy as jnp
from jax import lax
from jax.experimental import pallas as pl
from jax.sharding import Mesh, PartitionSpec as P

HD = 128


def attention_block(query, keys, values):
    seq, width = query.shape
    heads = width // HD
    qshaped = query.reshape(seq, heads, HD)
    kshaped = keys.reshape(seq, heads, HD)
    vshaped = values.reshape(seq, heads, HD)
    scores = jnp.einsum("qhd,khd->hqk", qshaped, kshaped, preferred_element_type=jnp.float32)
    scores = scores * (1.0 / math.sqrt(HD))
    rows_idx = lax.broadcasted_iota(jnp.int32, (seq, seq), 0)
    cols_idx = lax.broadcasted_iota(jnp.int32, (seq, seq), 1)
    scores = jnp.where((rows_idx >= cols_idx)[None], scores, -1e30)
    highest = jnp.max(scores, axis=-1, keepdims=True)
    expo = jnp.exp(scores - highest)
    prob = (expo / jnp.sum(expo, axis=-1, keepdims=True)).astype(jnp.bfloat16)
    output = jnp.einsum("hqk,khd->qhd", prob, vshaped, preferred_element_type=jnp.float32)
    return output.astype(jnp.bfloat16).reshape(seq, width)


def ring_pieces(block, axis):
    n = 4
    to_right = [(i, (i + 1) % n) for i in range(n)]
    to_left = [(i, (i - 1) % n) for i in range(n)]
    from_left = lax.ppermute(block, axis, to_right)
    from_right = lax.ppermute(block, axis, to_left)
    half = block.shape[1] // 2
    far_low = lax.ppermute(from_left[:, :half], axis, to_right)
    far_high = lax.ppermute(from_right[:, half:], axis, to_left)
    return block, from_right, far_low, far_high, from_left


def pieces_kernel(a_ref, w0_ref, w1_ref, w2lo_ref, w2hi_ref, w3_ref, lo_ref, hi_ref):
    k = w0_ref.shape[0]
    half = w2lo_ref.shape[1]
    a = a_ref[...]
    base = jnp.dot(a[:, 0:k], w0_ref[...], preferred_element_type=jnp.float32)
    base = base + jnp.dot(a[:, k:2 * k], w1_ref[...], preferred_element_type=jnp.float32)
    base = base + jnp.dot(a[:, 3 * k:4 * k], w3_ref[...], preferred_element_type=jnp.float32)
    far = a[:, 2 * k:3 * k]
    lo_ref[...] = base[:, 0:half] + jnp.dot(far, w2lo_ref[...], preferred_element_type=jnp.float32)
    hi_ref[...] = base[:, half:] + jnp.dot(far, w2hi_ref[...], preferred_element_type=jnp.float32)


def dot_pieces(a, pieces, tile=128):
    m, kk = a.shape
    n = pieces[0].shape[1]
    full = lambda p: pl.BlockSpec(p.shape, lambda i: (0, 0))
    half_spec = pl.BlockSpec((tile, n // 2), lambda i: (i, 0))
    half_shape = jax.ShapeDtypeStruct((m, n // 2), jnp.float32)
    return pl.pallas_call(
        pieces_kernel,
        grid=(m // tile,),
        in_specs=[pl.BlockSpec((tile, kk), lambda i: (i, 0))] + [full(p) for p in pieces],
        out_specs=(half_spec, half_spec),
        out_shape=(half_shape, half_shape),
        cost_estimate=pl.CostEstimate(
            flops=2 * m * kk * n, transcendentals=0, bytes_accessed=a.size * 2 + sum(p.size * 2 for p in pieces) + m * n * 4
        ),
    )(a, *pieces)


def ring_reduce_scatter(x, axis, n):
    me = lax.axis_index(axis)
    half = x.shape[2] // 2
    out = []
    for step_dir, cols in ((1, slice(0, half)), (-1, slice(half, None))):
        part = x[:, :, cols]
        perm = [(i, (i + step_dir) % n) for i in range(n)]
        acc = lax.dynamic_index_in_dim(part, (me - step_dir) % n, 0, keepdims=False)
        for k in range(n - 1):
            got = lax.ppermute(acc, axis, perm)
            seg = (me - step_dir * (k + 2)) % n
            acc = got + lax.dynamic_index_in_dim(part, seg, 0, keepdims=False)
        out.append(acc)
    return jnp.concatenate(out, axis=1)


def per_device(q_seq, k_seq, v_seq, resid, ln_gain, w_up, n_x):
    pieces = ring_pieces(w_up, "rx")
    attended = attention_block(q_seq, k_seq, v_seq)
    both = jnp.stack([resid, attended], axis=1)
    both = lax.all_to_all(both, "col", split_axis=0, concat_axis=1, tiled=True)
    chunk = both.shape[0]
    both = both.reshape(chunk, -1, 2, resid.shape[1])
    stream = (both[:, :, 0].astype(jnp.float32) + both[:, :, 1].astype(jnp.float32)).reshape(chunk, -1)
    full_width = stream.shape[1]
    mean = jnp.sum(stream, axis=1, keepdims=True) / full_width
    spread = jnp.sum(stream * stream, axis=1, keepdims=True) / full_width - mean * mean
    normed = ((stream - mean) * lax.rsqrt(spread + 1e-05) * ln_gain[None, :]).astype(jnp.bfloat16)
    block = w_up.shape[0]
    n_y = full_width // (n_x * block)
    grouped = normed.reshape(chunk, n_y, n_x, block)
    doubled = jnp.concatenate([grouped, grouped], axis=2)
    rolled = lax.dynamic_slice_in_dim(doubled, lax.axis_index("rx"), n_x, axis=2).reshape(chunk, full_width)
    part = lax.all_to_all(rolled, "ry", split_axis=1, concat_axis=0, tiled=True)
    part = part.reshape(n_y, chunk, part.shape[1])
    tokens = lax.all_gather(part, "col", axis=1, tiled=True)
    tokens = tokens.reshape(-1, tokens.shape[-1])
    low, high = dot_pieces(tokens, pieces)
    product_low = lax.psum_scatter(low, "ry", scatter_dimension=0, tiled=True)
    product_high = ring_reduce_scatter(high.reshape(n_y, -1, high.shape[1]), "ry", n_y)
    product = jnp.concatenate([product_low, product_high], axis=1)
    return jax.nn.gelu(product, approximate=True).astype(jnp.bfloat16)


def solution(mesh):
    n_row, n_col = mesh.shape["row"], mesh.shape["col"]
    nx = len({d.coords[0] for d in mesh.devices[:, 0]})
    split = Mesh(mesh.devices.reshape(n_row // nx, nx, n_col), ("ry", "rx", "col"))
    rows = ("ry", "rx")
    placed = (
        P(rows, "col"),
        P(rows, "col"),
        P(rows, "col"),
        P(rows, "col"),
        P(),
        P(rows, "col"),
    )

    def body(q_seq, k_seq, v_seq, resid, ln_gain, w_up):
        return per_device(q_seq, k_seq, v_seq, resid, ln_gain, w_up, nx)

    return jax.shard_map(body, mesh=split, in_specs=placed, out_specs=P(rows, "col"), check_vma=False)
```

```python
import math

import jax
import jax.numpy as jnp
from jax import lax
from jax.experimental import pallas as pl
from jax.sharding import Mesh, PartitionSpec as P

HD = 128


def attention_block(query, keys, values):
    seq, width = query.shape
    heads = width // HD
    qshaped = query.reshape(seq, heads, HD)
    kshaped = keys.reshape(seq, heads, HD)
    vshaped = values.reshape(seq, heads, HD)
    scores = jnp.einsum("qhd,khd->hqk", qshaped, kshaped, preferred_element_type=jnp.float32)
    scores = scores * (1.0 / math.sqrt(HD))
    rows_idx = lax.broadcasted_iota(jnp.int32, (seq, seq), 0)
    cols_idx = lax.broadcasted_iota(jnp.int32, (seq, seq), 1)
    scores = jnp.where((rows_idx >= cols_idx)[None], scores, -1e30)
    highest = jnp.max(scores, axis=-1, keepdims=True)
    expo = jnp.exp(scores - highest)
    prob = (expo / jnp.sum(expo, axis=-1, keepdims=True)).astype(jnp.bfloat16)
    output = jnp.einsum("hqk,khd->qhd", prob, vshaped, preferred_element_type=jnp.float32)
    return output.astype(jnp.bfloat16).reshape(seq, width)


def ring_pieces(block, axis):
    n = 4
    to_right = [(i, (i + 1) % n) for i in range(n)]
    to_left = [(i, (i - 1) % n) for i in range(n)]
    from_left = lax.ppermute(block, axis, to_right)
    from_right = lax.ppermute(block, axis, to_left)
    half = block.shape[1] // 2
    far_low = lax.ppermute(from_left[:, :half], axis, to_right)
    far_high = lax.ppermute(from_right[:, half:], axis, to_left)
    return block, from_right, far_low, far_high, from_left


def pieces_kernel(a_ref, w0_ref, w1_ref, w2lo_ref, w2hi_ref, w3_ref, lo_ref, hi_ref):
    k = w0_ref.shape[0]
    half = w2lo_ref.shape[1]
    a = a_ref[...]
    base = jnp.dot(a[:, 0:k], w0_ref[...], preferred_element_type=jnp.float32)
    base = base + jnp.dot(a[:, k:2 * k], w1_ref[...], preferred_element_type=jnp.float32)
    base = base + jnp.dot(a[:, 3 * k:4 * k], w3_ref[...], preferred_element_type=jnp.float32)
    far = a[:, 2 * k:3 * k]
    lo_ref[...] = base[:, 0:half] + jnp.dot(far, w2lo_ref[...], preferred_element_type=jnp.float32)
    hi_ref[...] = base[:, half:] + jnp.dot(far, w2hi_ref[...], preferred_element_type=jnp.float32)


def dot_pieces(a, pieces, tile=128):
    m, kk = a.shape
    n = pieces[0].shape[1]
    full = lambda p: pl.BlockSpec(p.shape, lambda i: (0, 0))
    half_spec = pl.BlockSpec((tile, n // 2), lambda i: (i, 0))
    half_shape = jax.ShapeDtypeStruct((m, n // 2), jnp.float32)
    return pl.pallas_call(
        pieces_kernel,
        grid=(m // tile,),
        in_specs=[pl.BlockSpec((tile, kk), lambda i: (i, 0))] + [full(p) for p in pieces],
        out_specs=(half_spec, half_spec),
        out_shape=(half_shape, half_shape),
        cost_estimate=pl.CostEstimate(
            flops=2 * m * kk * n, transcendentals=0, bytes_accessed=a.size * 2 + sum(p.size * 2 for p in pieces) + m * n * 4
        ),
    )(a, *pieces)


def ring_reduce_scatter(x, axis, n):
    me = lax.axis_index(axis)
    half = x.shape[2] // 2
    out = []
    for step_dir, cols in ((1, slice(0, half)), (-1, slice(half, None))):
        part = x[:, :, cols]
        perm = [(i, (i + step_dir) % n) for i in range(n)]
        acc = lax.dynamic_index_in_dim(part, (me - step_dir) % n, 0, keepdims=False)
        for k in range(n - 1):
            got = lax.ppermute(acc, axis, perm)
            seg = (me - step_dir * (k + 2)) % n
            acc = got + lax.dynamic_index_in_dim(part, seg, 0, keepdims=False)
        out.append(acc)
    return jnp.concatenate(out, axis=1)


def per_device(q_seq, k_seq, v_seq, resid, ln_gain, w_up, n_x):
    pieces = ring_pieces(w_up, "rx")
    attended = attention_block(q_seq, k_seq, v_seq)
    both = jnp.stack([resid, attended], axis=1)
    both = lax.all_to_all(both, "col", split_axis=0, concat_axis=1, tiled=True)
    chunk = both.shape[0]
    both = both.reshape(chunk, -1, 2, resid.shape[1])
    stream = (both[:, :, 0].astype(jnp.float32) + both[:, :, 1].astype(jnp.float32)).reshape(chunk, -1)
    full_width = stream.shape[1]
    mean = jnp.sum(stream, axis=1, keepdims=True) / full_width
    spread = jnp.sum(stream * stream, axis=1, keepdims=True) / full_width - mean * mean
    normed = ((stream - mean) * lax.rsqrt(spread + 1e-05) * ln_gain[None, :]).astype(jnp.bfloat16)
    block = w_up.shape[0]
    n_y = full_width // (n_x * block)
    grouped = normed.reshape(chunk, n_y, n_x, block)
    doubled = jnp.concatenate([grouped, grouped], axis=2)
    rolled = lax.dynamic_slice_in_dim(doubled, lax.axis_index("rx"), n_x, axis=2).reshape(chunk, full_width)
    part = lax.all_to_all(rolled, "ry", split_axis=1, concat_axis=0, tiled=True)
    part = part.reshape(n_y, chunk, part.shape[1])
    n_col = lax.axis_size("col")
    spread_out = jnp.broadcast_to(part[:, None], (part.shape[0], n_col) + part.shape[1:])
    tokens = lax.all_to_all(spread_out, "col", split_axis=1, concat_axis=1, tiled=True)
    tokens = tokens.reshape(-1, tokens.shape[-1])
    low, high = dot_pieces(tokens, pieces)
    partial = jnp.concatenate([low, high], axis=1)
    product = ring_reduce_scatter(partial.reshape(n_y, -1, partial.shape[1]), "ry", n_y)
    return jax.nn.gelu(product, approximate=True).astype(jnp.bfloat16)


def solution(mesh):
    n_row, n_col = mesh.shape["row"], mesh.shape["col"]
    nx = len({d.coords[0] for d in mesh.devices[:, 0]})
    split = Mesh(mesh.devices.reshape(n_row // nx, nx, n_col), ("ry", "rx", "col"))
    rows = ("ry", "rx")
    placed = (
        P(rows, "col"),
        P(rows, "col"),
        P(rows, "col"),
        P(rows, "col"),
        P(),
        P(rows, "col"),
    )

    def body(q_seq, k_seq, v_seq, resid, ln_gain, w_up):
        return per_device(q_seq, k_seq, v_seq, resid, ln_gain, w_up, nx)

    return jax.shard_map(body, mesh=split, in_specs=placed, out_specs=P(rows, "col"), check_vma=False)
```

```python
import math

import jax
import jax.numpy as jnp
from jax import lax
from jax.experimental import pallas as pl
from jax.sharding import Mesh, PartitionSpec as P

HD = 128


def attention_block(query, keys, values):
    seq, width = query.shape
    heads = width // HD
    qshaped = query.reshape(seq, heads, HD)
    kshaped = keys.reshape(seq, heads, HD)
    vshaped = values.reshape(seq, heads, HD)
    scores = jnp.einsum("qhd,khd->hqk", qshaped, kshaped, preferred_element_type=jnp.float32)
    scores = scores * (1.0 / math.sqrt(HD))
    rows_idx = lax.broadcasted_iota(jnp.int32, (seq, seq), 0)
    cols_idx = lax.broadcasted_iota(jnp.int32, (seq, seq), 1)
    scores = jnp.where((rows_idx >= cols_idx)[None], scores, -1e30)
    highest = jnp.max(scores, axis=-1, keepdims=True)
    expo = jnp.exp(scores - highest)
    prob = (expo / jnp.sum(expo, axis=-1, keepdims=True)).astype(jnp.bfloat16)
    output = jnp.einsum("hqk,khd->qhd", prob, vshaped, preferred_element_type=jnp.float32)
    return output.astype(jnp.bfloat16).reshape(seq, width)


def ring_pieces(block, axis):
    n = 4
    to_right = [(i, (i + 1) % n) for i in range(n)]
    to_left = [(i, (i - 1) % n) for i in range(n)]
    from_left = lax.ppermute(block, axis, to_right)
    from_right = lax.ppermute(block, axis, to_left)
    half = block.shape[1] // 2
    far_low = lax.ppermute(from_left[:, :half], axis, to_right)
    far_high = lax.ppermute(from_right[:, half:], axis, to_left)
    return block, from_right, far_low, far_high, from_left


def pieces_kernel(a_ref, w0_ref, w1_ref, w2lo_ref, w2hi_ref, w3_ref, *o_refs):
    k = w0_ref.shape[0]
    half = w2lo_ref.shape[1]
    quarter = o_refs[0].shape[1]
    a = a_ref[...]
    base = jnp.dot(a[:, 0:k], w0_ref[...], preferred_element_type=jnp.float32)
    base = base + jnp.dot(a[:, k:2 * k], w1_ref[...], preferred_element_type=jnp.float32)
    base = base + jnp.dot(a[:, 3 * k:4 * k], w3_ref[...], preferred_element_type=jnp.float32)
    far = a[:, 2 * k:3 * k]
    low = base[:, 0:half] + jnp.dot(far, w2lo_ref[...], preferred_element_type=jnp.float32)
    high = base[:, half:] + jnp.dot(far, w2hi_ref[...], preferred_element_type=jnp.float32)
    for q, o_ref in enumerate(o_refs):
        source = low if q < 2 else high
        start = (q % 2) * quarter
        o_ref[...] = source[:, start:start + quarter]


def dot_pieces(a, pieces, tile=128):
    m, kk = a.shape
    n = pieces[0].shape[1]
    full = lambda p: pl.BlockSpec(p.shape, lambda i: (0, 0))
    spec = pl.BlockSpec((tile, n // 4), lambda i: (i, 0))
    shape = jax.ShapeDtypeStruct((m, n // 4), jnp.float32)
    return pl.pallas_call(
        pieces_kernel,
        grid=(m // tile,),
        in_specs=[pl.BlockSpec((tile, kk), lambda i: (i, 0))] + [full(p) for p in pieces],
        out_specs=(spec,) * 4,
        out_shape=(shape,) * 4,
        cost_estimate=pl.CostEstimate(
            flops=2 * m * kk * n, transcendentals=0, bytes_accessed=a.size * 2 + sum(p.size * 2 for p in pieces) + m * n * 4
        ),
    )(a, *pieces)


def ring_reduce_scatter(parts, axis, n):
    me = lax.axis_index(axis)
    out = []
    for index, part in enumerate(parts):
        step_dir = 1 if index % 2 == 0 else -1
        perm = [(i, (i + step_dir) % n) for i in range(n)]
        acc = lax.dynamic_index_in_dim(part, (me - step_dir) % n, 0, keepdims=False)
        for k in range(n - 1):
            got = lax.ppermute(acc, axis, perm)
            seg = (me - step_dir * (k + 2)) % n
            acc = got + lax.dynamic_index_in_dim(part, seg, 0, keepdims=False)
        out.append(acc)
    return jnp.concatenate(out, axis=1)


def per_device(q_seq, k_seq, v_seq, resid, ln_gain, w_up, n_x):
    pieces = ring_pieces(w_up, "rx")
    attended = attention_block(q_seq, k_seq, v_seq)
    both = jnp.stack([resid, attended], axis=1)
    both = lax.all_to_all(both, "col", split_axis=0, concat_axis=1, tiled=True)
    chunk = both.shape[0]
    both = both.reshape(chunk, -1, 2, resid.shape[1])
    stream = (both[:, :, 0].astype(jnp.float32) + both[:, :, 1].astype(jnp.float32)).reshape(chunk, -1)
    full_width = stream.shape[1]
    mean = jnp.sum(stream, axis=1, keepdims=True) / full_width
    spread = jnp.sum(stream * stream, axis=1, keepdims=True) / full_width - mean * mean
    normed = ((stream - mean) * lax.rsqrt(spread + 1e-05) * ln_gain[None, :]).astype(jnp.bfloat16)
    block = w_up.shape[0]
    n_y = full_width // (n_x * block)
    grouped = normed.reshape(chunk, n_y, n_x, block)
    doubled = jnp.concatenate([grouped, grouped], axis=2)
    rolled = lax.dynamic_slice_in_dim(doubled, lax.axis_index("rx"), n_x, axis=2).reshape(chunk, full_width)
    part = lax.all_to_all(rolled, "ry", split_axis=1, concat_axis=0, tiled=True)
    part = part.reshape(n_y, chunk, part.shape[1])
    n_col = lax.axis_size("col")
    spread_out = jnp.broadcast_to(part[:, None], (part.shape[0], n_col) + part.shape[1:])
    tokens = lax.all_to_all(spread_out, "col", split_axis=1, concat_axis=1, tiled=True)
    tokens = tokens.reshape(-1, tokens.shape[-1])
    quarters = dot_pieces(tokens, pieces)
    product = ring_reduce_scatter([q.reshape(n_y, -1, q.shape[1]) for q in quarters], "ry", n_y)
    return jax.nn.gelu(product, approximate=True).astype(jnp.bfloat16)


def solution(mesh):
    n_row, n_col = mesh.shape["row"], mesh.shape["col"]
    nx = len({d.coords[0] for d in mesh.devices[:, 0]})
    split = Mesh(mesh.devices.reshape(n_row // nx, nx, n_col), ("ry", "rx", "col"))
    rows = ("ry", "rx")
    placed = (
        P(rows, "col"),
        P(rows, "col"),
        P(rows, "col"),
        P(rows, "col"),
        P(),
        P(rows, "col"),
    )

    def body(q_seq, k_seq, v_seq, resid, ln_gain, w_up):
        return per_device(q_seq, k_seq, v_seq, resid, ln_gain, w_up, nx)

    return jax.shard_map(body, mesh=split, in_specs=placed, out_specs=P(rows, "col"), check_vma=False)
```

```python
import math

import jax
import jax.numpy as jnp
from jax import lax
from jax.experimental import pallas as pl
from jax.sharding import Mesh, PartitionSpec as P

HD = 128


def attention_block(query, keys, values):
    seq, width = query.shape
    rows_idx = lax.broadcasted_iota(jnp.int32, (seq, seq), 0)
    cols_idx = lax.broadcasted_iota(jnp.int32, (seq, seq), 1)
    causal = rows_idx >= cols_idx
    outputs = []
    for head in range(width // HD):
        cols = slice(head * HD, (head + 1) * HD)
        scores = lax.dot_general(
            query[:, cols], keys[:, cols], (((1,), (1,)), ((), ())), preferred_element_type=jnp.float32
        )
        scores = scores * (1.0 / math.sqrt(HD))
        scores = jnp.where(causal, scores, -1e30)
        highest = jnp.max(scores, axis=-1, keepdims=True)
        expo = jnp.exp(scores - highest)
        prob = (expo / jnp.sum(expo, axis=-1, keepdims=True)).astype(jnp.bfloat16)
        output = jnp.dot(prob, values[:, cols], preferred_element_type=jnp.float32)
        outputs.append(output.astype(jnp.bfloat16))
    return jnp.concatenate(outputs, axis=1)


def ring_pieces(block, axis):
    n = 4
    to_right = [(i, (i + 1) % n) for i in range(n)]
    to_left = [(i, (i - 1) % n) for i in range(n)]
    from_left = lax.ppermute(block, axis, to_right)
    from_right = lax.ppermute(block, axis, to_left)
    half = block.shape[1] // 2
    far_low = lax.ppermute(from_left[:, :half], axis, to_right)
    far_high = lax.ppermute(from_right[:, half:], axis, to_left)
    return block, from_right, far_low, far_high, from_left


def pieces_kernel(a_ref, w0_ref, w1_ref, w2lo_ref, w2hi_ref, w3_ref, *o_refs):
    k = w0_ref.shape[0]
    half = w2lo_ref.shape[1]
    quarter = o_refs[0].shape[1]
    a = a_ref[...]
    base = jnp.dot(a[:, 0:k], w0_ref[...], preferred_element_type=jnp.float32)
    base = base + jnp.dot(a[:, k:2 * k], w1_ref[...], preferred_element_type=jnp.float32)
    base = base + jnp.dot(a[:, 3 * k:4 * k], w3_ref[...], preferred_element_type=jnp.float32)
    far = a[:, 2 * k:3 * k]
    low = base[:, 0:half] + jnp.dot(far, w2lo_ref[...], preferred_element_type=jnp.float32)
    high = base[:, half:] + jnp.dot(far, w2hi_ref[...], preferred_element_type=jnp.float32)
    for q, o_ref in enumerate(o_refs):
        source = low if q < 2 else high
        start = (q % 2) * quarter
        o_ref[...] = source[:, start:start + quarter]


def dot_pieces(a, pieces, tile=128):
    m, kk = a.shape
    n = pieces[0].shape[1]
    full = lambda p: pl.BlockSpec(p.shape, lambda i: (0, 0))
    spec = pl.BlockSpec((tile, n // 4), lambda i: (i, 0))
    shape = jax.ShapeDtypeStruct((m, n // 4), jnp.float32)
    return pl.pallas_call(
        pieces_kernel,
        grid=(m // tile,),
        in_specs=[pl.BlockSpec((tile, kk), lambda i: (i, 0))] + [full(p) for p in pieces],
        out_specs=(spec,) * 4,
        out_shape=(shape,) * 4,
        cost_estimate=pl.CostEstimate(
            flops=2 * m * kk * n, transcendentals=0, bytes_accessed=a.size * 2 + sum(p.size * 2 for p in pieces) + m * n * 4
        ),
    )(a, *pieces)


def ring_reduce_scatter(parts, axis, n):
    me = lax.axis_index(axis)
    out = []
    for index, part in enumerate(parts):
        step_dir = 1 if index % 2 == 0 else -1
        perm = [(i, (i + step_dir) % n) for i in range(n)]
        acc = lax.dynamic_index_in_dim(part, (me - step_dir) % n, 0, keepdims=False)
        for k in range(n - 1):
            got = lax.ppermute(acc, axis, perm)
            seg = (me - step_dir * (k + 2)) % n
            acc = got + lax.dynamic_index_in_dim(part, seg, 0, keepdims=False)
        out.append(acc)
    return jnp.concatenate(out, axis=1)


def per_device(q_seq, k_seq, v_seq, resid, ln_gain, w_up, n_x):
    pieces = ring_pieces(w_up, "rx")
    attended = attention_block(q_seq, k_seq, v_seq)
    both = jnp.stack([resid, attended], axis=1)
    both = lax.all_to_all(both, "col", split_axis=0, concat_axis=1, tiled=True)
    chunk = both.shape[0]
    both = both.reshape(chunk, -1, 2, resid.shape[1])
    stream = (both[:, :, 0].astype(jnp.float32) + both[:, :, 1].astype(jnp.float32)).reshape(chunk, -1)
    full_width = stream.shape[1]
    mean = jnp.sum(stream, axis=1, keepdims=True) / full_width
    spread = jnp.sum(stream * stream, axis=1, keepdims=True) / full_width - mean * mean
    normed = ((stream - mean) * lax.rsqrt(spread + 1e-05) * ln_gain[None, :]).astype(jnp.bfloat16)
    block = w_up.shape[0]
    n_y = full_width // (n_x * block)
    grouped = normed.reshape(chunk, n_y, n_x, block)
    doubled = jnp.concatenate([grouped, grouped], axis=2)
    rolled = lax.dynamic_slice_in_dim(doubled, lax.axis_index("rx"), n_x, axis=2).reshape(chunk, full_width)
    part = lax.all_to_all(rolled, "ry", split_axis=1, concat_axis=0, tiled=True)
    part = part.reshape(n_y, chunk, part.shape[1])
    n_col = lax.axis_size("col")
    spread_out = jnp.broadcast_to(part[:, None], (part.shape[0], n_col) + part.shape[1:])
    tokens = lax.all_to_all(spread_out, "col", split_axis=1, concat_axis=1, tiled=True)
    tokens = tokens.reshape(-1, tokens.shape[-1])
    quarters = dot_pieces(tokens, pieces)
    product = ring_reduce_scatter([q.reshape(n_y, -1, q.shape[1]) for q in quarters], "ry", n_y)
    return jax.nn.gelu(product, approximate=True).astype(jnp.bfloat16)


def solution(mesh):
    n_row, n_col = mesh.shape["row"], mesh.shape["col"]
    nx = len({d.coords[0] for d in mesh.devices[:, 0]})
    split = Mesh(mesh.devices.reshape(n_row // nx, nx, n_col), ("ry", "rx", "col"))
    rows = ("ry", "rx")
    placed = (
        P(rows, "col"),
        P(rows, "col"),
        P(rows, "col"),
        P(rows, "col"),
        P(),
        P(rows, "col"),
    )

    def body(q_seq, k_seq, v_seq, resid, ln_gain, w_up):
        return per_device(q_seq, k_seq, v_seq, resid, ln_gain, w_up, nx)

    return jax.shard_map(body, mesh=split, in_specs=placed, out_specs=P(rows, "col"), check_vma=False)
```

```python
import math

import jax
import jax.numpy as jnp
from jax import lax
from jax.experimental import pallas as pl
from jax.sharding import Mesh, PartitionSpec as P

HD = 128


def attention_block(query, keys, values):
    seq, width = query.shape
    heads = width // HD
    qshaped = query.reshape(seq, heads, HD)
    kshaped = keys.reshape(seq, heads, HD)
    vshaped = values.reshape(seq, heads, HD)
    scores = jnp.einsum("qhd,khd->hqk", qshaped, kshaped, preferred_element_type=jnp.float32)
    scores = scores * (1.0 / math.sqrt(HD))
    rows_idx = lax.broadcasted_iota(jnp.int32, (seq, seq), 0)
    cols_idx = lax.broadcasted_iota(jnp.int32, (seq, seq), 1)
    scores = jnp.where((rows_idx >= cols_idx)[None], scores, -1e30)
    highest = jnp.max(scores, axis=-1, keepdims=True)
    expo = jnp.exp(scores - highest)
    prob = (expo / jnp.sum(expo, axis=-1, keepdims=True)).astype(jnp.bfloat16)
    output = jnp.einsum("hqk,khd->qhd", prob, vshaped, preferred_element_type=jnp.float32)
    return output.astype(jnp.bfloat16).reshape(seq, width)


def ring_pieces(block, axis):
    n = 4
    to_right = [(i, (i + 1) % n) for i in range(n)]
    to_left = [(i, (i - 1) % n) for i in range(n)]
    from_left = lax.ppermute(block, axis, to_right)
    from_right = lax.ppermute(block, axis, to_left)
    half = block.shape[1] // 2
    far_low = lax.ppermute(from_left[:, :half], axis, to_right)
    far_high = lax.ppermute(from_right[:, half:], axis, to_left)
    return block, from_right, far_low, far_high, from_left


def pieces_kernel(a_ref, w0_ref, w1_ref, w2lo_ref, w2hi_ref, w3_ref, *o_refs):
    k = w0_ref.shape[0]
    half = w2lo_ref.shape[1]
    quarter = o_refs[0].shape[1]
    a = a_ref[...]
    base = jnp.dot(a[:, 0:k], w0_ref[...], preferred_element_type=jnp.float32)
    base = base + jnp.dot(a[:, k:2 * k], w1_ref[...], preferred_element_type=jnp.float32)
    base = base + jnp.dot(a[:, 3 * k:4 * k], w3_ref[...], preferred_element_type=jnp.float32)
    far = a[:, 2 * k:3 * k]
    low = base[:, 0:half] + jnp.dot(far, w2lo_ref[...], preferred_element_type=jnp.float32)
    high = base[:, half:] + jnp.dot(far, w2hi_ref[...], preferred_element_type=jnp.float32)
    for q, o_ref in enumerate(o_refs):
        source = low if q < 2 else high
        start = (q % 2) * quarter
        o_ref[...] = source[:, start:start + quarter]


def dot_pieces(a, pieces, tile=256):
    m, kk = a.shape
    n = pieces[0].shape[1]
    full = lambda p: pl.BlockSpec(p.shape, lambda i: (0, 0))
    spec = pl.BlockSpec((tile, n // 4), lambda i: (i, 0))
    shape = jax.ShapeDtypeStruct((m, n // 4), jnp.float32)
    return pl.pallas_call(
        pieces_kernel,
        grid=(m // tile,),
        in_specs=[pl.BlockSpec((tile, kk), lambda i: (i, 0))] + [full(p) for p in pieces],
        out_specs=(spec,) * 4,
        out_shape=(shape,) * 4,
        cost_estimate=pl.CostEstimate(
            flops=2 * m * kk * n, transcendentals=0, bytes_accessed=a.size * 2 + sum(p.size * 2 for p in pieces) + m * n * 4
        ),
    )(a, *pieces)


def ring_reduce_scatter(parts, axis, n):
    me = lax.axis_index(axis)
    out = []
    for index, part in enumerate(parts):
        step_dir = 1 if index % 2 == 0 else -1
        perm = [(i, (i + step_dir) % n) for i in range(n)]
        acc = lax.dynamic_index_in_dim(part, (me - step_dir) % n, 0, keepdims=False)
        for k in range(n - 1):
            got = lax.ppermute(acc, axis, perm)
            seg = (me - step_dir * (k + 2)) % n
            acc = got + lax.dynamic_index_in_dim(part, seg, 0, keepdims=False)
        out.append(acc)
    return jnp.concatenate(out, axis=1)


def per_device(q_seq, k_seq, v_seq, resid, ln_gain, w_up, n_x):
    pieces = ring_pieces(w_up, "rx")
    attended = attention_block(q_seq, k_seq, v_seq)
    both = jnp.stack([resid, attended], axis=1)
    both = lax.all_to_all(both, "col", split_axis=0, concat_axis=1, tiled=True)
    chunk = both.shape[0]
    both = both.reshape(chunk, -1, 2, resid.shape[1])
    stream = (both[:, :, 0].astype(jnp.float32) + both[:, :, 1].astype(jnp.float32)).reshape(chunk, -1)
    full_width = stream.shape[1]
    mean = jnp.sum(stream, axis=1, keepdims=True) / full_width
    spread = jnp.sum(stream * stream, axis=1, keepdims=True) / full_width - mean * mean
    normed = ((stream - mean) * lax.rsqrt(spread + 1e-05) * ln_gain[None, :]).astype(jnp.bfloat16)
    block = w_up.shape[0]
    n_y = full_width // (n_x * block)
    grouped = normed.reshape(chunk, n_y, n_x, block)
    doubled = jnp.concatenate([grouped, grouped], axis=2)
    rolled = lax.dynamic_slice_in_dim(doubled, lax.axis_index("rx"), n_x, axis=2).reshape(chunk, full_width)
    part = lax.all_to_all(rolled, "ry", split_axis=1, concat_axis=0, tiled=True)
    part = part.reshape(n_y, chunk, part.shape[1])
    n_col = lax.axis_size("col")
    spread_out = jnp.broadcast_to(part[:, None], (part.shape[0], n_col) + part.shape[1:])
    tokens = lax.all_to_all(spread_out, "col", split_axis=1, concat_axis=1, tiled=True)
    tokens = tokens.reshape(-1, tokens.shape[-1])
    quarters = dot_pieces(tokens, pieces)
    product = ring_reduce_scatter([q.reshape(n_y, -1, q.shape[1]) for q in quarters], "ry", n_y)
    return jax.nn.gelu(product, approximate=True).astype(jnp.bfloat16)


def solution(mesh):
    n_row, n_col = mesh.shape["row"], mesh.shape["col"]
    nx = len({d.coords[0] for d in mesh.devices[:, 0]})
    split = Mesh(mesh.devices.reshape(n_row // nx, nx, n_col), ("ry", "rx", "col"))
    rows = ("ry", "rx")
    placed = (
        P(rows, "col"),
        P(rows, "col"),
        P(rows, "col"),
        P(rows, "col"),
        P(),
        P(rows, "col"),
    )

    def body(q_seq, k_seq, v_seq, resid, ln_gain, w_up):
        return per_device(q_seq, k_seq, v_seq, resid, ln_gain, w_up, nx)

    return jax.shard_map(body, mesh=split, in_specs=placed, out_specs=P(rows, "col"), check_vma=False)
```

```python
import math

import jax
import jax.numpy as jnp
from jax import lax
from jax.experimental import pallas as pl
from jax.sharding import Mesh, PartitionSpec as P

HD = 128


def attention_block(query, keys, values):
    seq, width = query.shape
    heads = width // HD
    qshaped = query.reshape(seq, heads, HD)
    kshaped = keys.reshape(seq, heads, HD)
    vshaped = values.reshape(seq, heads, HD)
    scores = jnp.einsum("qhd,khd->hqk", qshaped, kshaped, preferred_element_type=jnp.float32)
    scores = scores * (1.0 / math.sqrt(HD))
    rows_idx = lax.broadcasted_iota(jnp.int32, (seq, seq), 0)
    cols_idx = lax.broadcasted_iota(jnp.int32, (seq, seq), 1)
    scores = jnp.where((rows_idx >= cols_idx)[None], scores, -1e30)
    highest = jnp.max(scores, axis=-1, keepdims=True)
    expo = jnp.exp(scores - highest)
    prob = (expo / jnp.sum(expo, axis=-1, keepdims=True)).astype(jnp.bfloat16)
    output = jnp.einsum("hqk,khd->qhd", prob, vshaped, preferred_element_type=jnp.float32)
    return output.astype(jnp.bfloat16).reshape(seq, width)


def ring_pieces(block, axis):
    n = 4
    to_right = [(i, (i + 1) % n) for i in range(n)]
    to_left = [(i, (i - 1) % n) for i in range(n)]
    from_left = lax.ppermute(block, axis, to_right)
    from_right = lax.ppermute(block, axis, to_left)
    half = block.shape[1] // 2
    far_low = lax.ppermute(from_left[:, :half], axis, to_right)
    far_high = lax.ppermute(from_right[:, half:], axis, to_left)
    return block, from_right, far_low, far_high, from_left


def near_kernel(a_ref, w0_ref, w1_ref, w3_ref, *o_refs):
    k = w0_ref.shape[0]
    quarter = o_refs[0].shape[1]
    a = a_ref[...]
    base = jnp.dot(a[:, 0:k], w0_ref[...], preferred_element_type=jnp.float32)
    base = base + jnp.dot(a[:, k:2 * k], w1_ref[...], preferred_element_type=jnp.float32)
    base = base + jnp.dot(a[:, 3 * k:4 * k], w3_ref[...], preferred_element_type=jnp.float32)
    for q, o_ref in enumerate(o_refs):
        o_ref[...] = base[:, q * quarter:(q + 1) * quarter]


def far_kernel(a_ref, w2lo_ref, w2hi_ref, *refs):
    k = w2lo_ref.shape[0]
    acc_refs, o_refs = refs[:4], refs[4:]
    quarter = o_refs[0].shape[1]
    far = a_ref[:, 2 * k:3 * k]
    low = jnp.dot(far, w2lo_ref[...], preferred_element_type=jnp.float32)
    high = jnp.dot(far, w2hi_ref[...], preferred_element_type=jnp.float32)
    for q, (acc_ref, o_ref) in enumerate(zip(acc_refs, o_refs)):
        source = low if q < 2 else high
        start = (q % 2) * quarter
        o_ref[...] = acc_ref[...] + source[:, start:start + quarter]


def dot_pieces(a, pieces, tile=256):
    m, kk = a.shape
    n = pieces[0].shape[1]
    own, right, far_low, far_high, left = pieces
    full = lambda p: pl.BlockSpec(p.shape, lambda i: (0, 0))
    spec = pl.BlockSpec((tile, n // 4), lambda i: (i, 0))
    shape = jax.ShapeDtypeStruct((m, n // 4), jnp.float32)
    a_spec = pl.BlockSpec((tile, kk), lambda i: (i, 0))
    near_w = (own, right, left)
    quarters = pl.pallas_call(
        near_kernel,
        grid=(m // tile,),
        in_specs=[a_spec] + [full(p) for p in near_w],
        out_specs=(spec,) * 4,
        out_shape=(shape,) * 4,
        cost_estimate=pl.CostEstimate(
            flops=2 * m * 3 * own.size, transcendentals=0, bytes_accessed=a.size * 2 + 3 * own.size * 2 + m * n * 4
        ),
    )(a, *near_w)
    return pl.pallas_call(
        far_kernel,
        grid=(m // tile,),
        in_specs=[a_spec, full(far_low), full(far_high)] + [spec] * 4,
        out_specs=(spec,) * 4,
        out_shape=(shape,) * 4,
        input_output_aliases={3: 0, 4: 1, 5: 2, 6: 3},
        cost_estimate=pl.CostEstimate(
            flops=2 * m * own.size, transcendentals=0, bytes_accessed=a.size * 2 + own.size * 2 + 2 * m * n * 4
        ),
    )(a, far_low, far_high, *quarters)


def ring_reduce_scatter(parts, axis, n):
    me = lax.axis_index(axis)
    out = []
    for index, part in enumerate(parts):
        step_dir = 1 if index % 2 == 0 else -1
        perm = [(i, (i + step_dir) % n) for i in range(n)]
        acc = lax.dynamic_index_in_dim(part, (me - step_dir) % n, 0, keepdims=False)
        for k in range(n - 1):
            got = lax.ppermute(acc, axis, perm)
            seg = (me - step_dir * (k + 2)) % n
            acc = got + lax.dynamic_index_in_dim(part, seg, 0, keepdims=False)
        out.append(acc)
    return jnp.concatenate(out, axis=1)


def per_device(q_seq, k_seq, v_seq, resid, ln_gain, w_up, n_x):
    pieces = ring_pieces(w_up, "rx")
    attended = attention_block(q_seq, k_seq, v_seq)
    both = jnp.stack([resid, attended], axis=1)
    both = lax.all_to_all(both, "col", split_axis=0, concat_axis=1, tiled=True)
    chunk = both.shape[0]
    both = both.reshape(chunk, -1, 2, resid.shape[1])
    stream = (both[:, :, 0].astype(jnp.float32) + both[:, :, 1].astype(jnp.float32)).reshape(chunk, -1)
    full_width = stream.shape[1]
    mean = jnp.sum(stream, axis=1, keepdims=True) / full_width
    spread = jnp.sum(stream * stream, axis=1, keepdims=True) / full_width - mean * mean
    normed = ((stream - mean) * lax.rsqrt(spread + 1e-05) * ln_gain[None, :]).astype(jnp.bfloat16)
    block = w_up.shape[0]
    n_y = full_width // (n_x * block)
    grouped = normed.reshape(chunk, n_y, n_x, block)
    doubled = jnp.concatenate([grouped, grouped], axis=2)
    rolled = lax.dynamic_slice_in_dim(doubled, lax.axis_index("rx"), n_x, axis=2).reshape(chunk, full_width)
    part = lax.all_to_all(rolled, "ry", split_axis=1, concat_axis=0, tiled=True)
    part = part.reshape(n_y, chunk, part.shape[1])
    n_col = lax.axis_size("col")
    spread_out = jnp.broadcast_to(part[:, None], (part.shape[0], n_col) + part.shape[1:])
    tokens = lax.all_to_all(spread_out, "col", split_axis=1, concat_axis=1, tiled=True)
    tokens = tokens.reshape(-1, tokens.shape[-1])
    quarters = dot_pieces(tokens, pieces)
    product = ring_reduce_scatter([q.reshape(n_y, -1, q.shape[1]) for q in quarters], "ry", n_y)
    return jax.nn.gelu(product, approximate=True).astype(jnp.bfloat16)


def solution(mesh):
    n_row, n_col = mesh.shape["row"], mesh.shape["col"]
    nx = len({d.coords[0] for d in mesh.devices[:, 0]})
    split = Mesh(mesh.devices.reshape(n_row // nx, nx, n_col), ("ry", "rx", "col"))
    rows = ("ry", "rx")
    placed = (
        P(rows, "col"),
        P(rows, "col"),
        P(rows, "col"),
        P(rows, "col"),
        P(),
        P(rows, "col"),
    )

    def body(q_seq, k_seq, v_seq, resid, ln_gain, w_up):
        return per_device(q_seq, k_seq, v_seq, resid, ln_gain, w_up, nx)

    return jax.shard_map(body, mesh=split, in_specs=placed, out_specs=P(rows, "col"), check_vma=False)
```

```python
import math

import jax
import jax.numpy as jnp
from jax import lax
from jax.experimental import pallas as pl
from jax.sharding import Mesh, PartitionSpec as P

HD = 128


def attention_block(query, keys, values):
    seq, width = query.shape
    heads = width // HD
    qshaped = query.reshape(seq, heads, HD)
    kshaped = keys.reshape(seq, heads, HD)
    vshaped = values.reshape(seq, heads, HD)
    scores = jnp.einsum("qhd,khd->hqk", qshaped, kshaped, preferred_element_type=jnp.float32)
    scores = scores * (1.0 / math.sqrt(HD))
    rows_idx = lax.broadcasted_iota(jnp.int32, (seq, seq), 0)
    cols_idx = lax.broadcasted_iota(jnp.int32, (seq, seq), 1)
    scores = jnp.where((rows_idx >= cols_idx)[None], scores, -1e30)
    highest = jnp.max(scores, axis=-1, keepdims=True)
    expo = jnp.exp(scores - highest)
    prob = (expo / jnp.sum(expo, axis=-1, keepdims=True)).astype(jnp.bfloat16)
    output = jnp.einsum("hqk,khd->qhd", prob, vshaped, preferred_element_type=jnp.float32)
    return output.astype(jnp.bfloat16).reshape(seq, width)


def ring_pieces(block, axis):
    n = 4
    to_right = [(i, (i + 1) % n) for i in range(n)]
    to_left = [(i, (i - 1) % n) for i in range(n)]
    from_left = lax.ppermute(block, axis, to_right)
    from_right = lax.ppermute(block, axis, to_left)
    half = block.shape[1] // 2
    far_low = lax.ppermute(from_left[:, :half], axis, to_right)
    far_high = lax.ppermute(from_right[:, half:], axis, to_left)
    return block, from_right, far_low, far_high, from_left


def near_kernel(a_ref, w0_ref, w1_ref, w3_ref, *o_refs):
    k = w0_ref.shape[0]
    quarter = o_refs[0].shape[1]
    a = a_ref[...]
    base = jnp.dot(a[:, 0:k], w0_ref[...], preferred_element_type=jnp.float32)
    base = base + jnp.dot(a[:, k:2 * k], w1_ref[...], preferred_element_type=jnp.float32)
    base = base + jnp.dot(a[:, 3 * k:4 * k], w3_ref[...], preferred_element_type=jnp.float32)
    for q, o_ref in enumerate(o_refs):
        o_ref[...] = base[:, q * quarter:(q + 1) * quarter]


def far_kernel(a_ref, w2lo_ref, w2hi_ref, *refs):
    k = w2lo_ref.shape[0]
    acc_refs, o_refs = refs[:4], refs[4:]
    quarter = o_refs[0].shape[1]
    far = a_ref[:, 2 * k:3 * k]
    low = jnp.dot(far, w2lo_ref[...], preferred_element_type=jnp.float32)
    high = jnp.dot(far, w2hi_ref[...], preferred_element_type=jnp.float32)
    for q, (acc_ref, o_ref) in enumerate(zip(acc_refs, o_refs)):
        source = low if q < 2 else high
        start = (q % 2) * quarter
        o_ref[...] = acc_ref[...] + source[:, start:start + quarter]


def dot_pieces(a, pieces, tile=256):
    m, kk = a.shape
    n = pieces[0].shape[1]
    own, right, far_low, far_high, left = pieces
    full = lambda p: pl.BlockSpec(p.shape, lambda i: (0, 0))
    spec = pl.BlockSpec((tile, n // 4), lambda i: (i, 0))
    shape = jax.ShapeDtypeStruct((m, n // 4), jnp.float32)
    a_spec = pl.BlockSpec((tile, kk), lambda i: (i, 0))
    near_w = (own, right, left)
    quarters = pl.pallas_call(
        near_kernel,
        grid=(m // tile,),
        in_specs=[a_spec] + [full(p) for p in near_w],
        out_specs=(spec,) * 4,
        out_shape=(shape,) * 4,
        cost_estimate=pl.CostEstimate(
            flops=2 * m * 3 * own.size, transcendentals=0, bytes_accessed=a.size * 2 + 3 * own.size * 2 + m * n * 4
        ),
    )(a, *near_w)
    return pl.pallas_call(
        far_kernel,
        grid=(m // tile,),
        in_specs=[a_spec, full(far_low), full(far_high)] + [spec] * 4,
        out_specs=(spec,) * 4,
        out_shape=(shape,) * 4,
        input_output_aliases={3: 0, 4: 1, 5: 2, 6: 3},
        cost_estimate=pl.CostEstimate(
            flops=2 * m * own.size, transcendentals=0, bytes_accessed=a.size * 2 + own.size * 2 + 2 * m * n * 4
        ),
    )(a, far_low, far_high, *quarters)


def ring_reduce_scatter(parts, axis, n):
    me = lax.axis_index(axis)
    out = []
    for index, part in enumerate(parts):
        step_dir = 1 if index % 2 == 0 else -1
        perm = [(i, (i + step_dir) % n) for i in range(n)]
        acc = lax.dynamic_index_in_dim(part, (me - step_dir) % n, 0, keepdims=False)
        for k in range(n - 1):
            got = lax.ppermute(acc, axis, perm)
            seg = (me - step_dir * (k + 2)) % n
            acc = got + lax.dynamic_index_in_dim(part, seg, 0, keepdims=False)
        out.append(acc)
    return jnp.concatenate(out, axis=1)


def per_device(q_seq, k_seq, v_seq, resid, ln_gain, w_up, n_x):
    pieces = ring_pieces(w_up, "rx")
    attended = attention_block(q_seq, k_seq, v_seq)
    both = jnp.stack([resid, attended], axis=1)
    both = lax.all_to_all(both, "col", split_axis=0, concat_axis=1, tiled=True)
    chunk = both.shape[0]
    both = both.reshape(chunk, -1, 2, resid.shape[1])
    stream = (both[:, :, 0].astype(jnp.float32) + both[:, :, 1].astype(jnp.float32)).reshape(chunk, -1)
    full_width = stream.shape[1]
    mean = jnp.sum(stream, axis=1, keepdims=True) / full_width
    spread = jnp.sum(stream * stream, axis=1, keepdims=True) / full_width - mean * mean
    normed = ((stream - mean) * lax.rsqrt(spread + 1e-05) * ln_gain[None, :]).astype(jnp.bfloat16)
    block = w_up.shape[0]
    n_y = full_width // (n_x * block)
    grouped = normed.reshape(chunk, n_y, n_x, block)
    doubled = jnp.concatenate([grouped, grouped], axis=2)
    rolled = lax.dynamic_slice_in_dim(doubled, lax.axis_index("rx"), n_x, axis=2).reshape(chunk, full_width)
    part = lax.all_to_all(rolled, "ry", split_axis=1, concat_axis=0, tiled=True)
    part = part.reshape(n_y, chunk, part.shape[1])
    n_col = lax.axis_size("col")
    spread_out = jnp.broadcast_to(part[:, None], (part.shape[0], n_col) + part.shape[1:])
    tokens = lax.all_to_all(spread_out, "col", split_axis=1, concat_axis=1, tiled=True)
    tokens = tokens.reshape(-1, tokens.shape[-1])
    quarters = dot_pieces(tokens, pieces)
    segments = [q.reshape(n_y, 2, -1, q.shape[1]) for q in quarters]
    halves = [seg[:, h] for seg in segments for h in range(2)]
    summed = ring_reduce_scatter(halves, "ry", n_y)
    width = quarters[0].shape[1]
    product = jnp.concatenate(
        [jnp.concatenate([summed[:, (2 * q) * width:(2 * q + 1) * width], summed[:, (2 * q + 1) * width:(2 * q + 2) * width]], axis=0)
         for q in range(4)],
        axis=1,
    )
    return jax.nn.gelu(product, approximate=True).astype(jnp.bfloat16)


def solution(mesh):
    n_row, n_col = mesh.shape["row"], mesh.shape["col"]
    nx = len({d.coords[0] for d in mesh.devices[:, 0]})
    split = Mesh(mesh.devices.reshape(n_row // nx, nx, n_col), ("ry", "rx", "col"))
    rows = ("ry", "rx")
    placed = (
        P(rows, "col"),
        P(rows, "col"),
        P(rows, "col"),
        P(rows, "col"),
        P(),
        P(rows, "col"),
    )

    def body(q_seq, k_seq, v_seq, resid, ln_gain, w_up):
        return per_device(q_seq, k_seq, v_seq, resid, ln_gain, w_up, nx)

    return jax.shard_map(body, mesh=split, in_specs=placed, out_specs=P(rows, "col"), check_vma=False)
```

```python
import math

import jax
import jax.numpy as jnp
from jax import lax
from jax.experimental import pallas as pl
from jax.sharding import Mesh, PartitionSpec as P

HD = 128


def attention_block(query, keys, values):
    seq, width = query.shape
    heads = width // HD
    qshaped = query.reshape(seq, heads, HD)
    kshaped = keys.reshape(seq, heads, HD)
    vshaped = values.reshape(seq, heads, HD)
    scores = jnp.einsum("qhd,khd->hqk", qshaped, kshaped, preferred_element_type=jnp.float32)
    scores = scores * (1.0 / math.sqrt(HD))
    rows_idx = lax.broadcasted_iota(jnp.int32, (seq, seq), 0)
    cols_idx = lax.broadcasted_iota(jnp.int32, (seq, seq), 1)
    scores = jnp.where((rows_idx >= cols_idx)[None], scores, -1e30)
    highest = jnp.max(scores, axis=-1, keepdims=True)
    expo = jnp.exp(scores - highest)
    prob = (expo / jnp.sum(expo, axis=-1, keepdims=True)).astype(jnp.bfloat16)
    output = jnp.einsum("hqk,khd->qhd", prob, vshaped, preferred_element_type=jnp.float32)
    return output.astype(jnp.bfloat16).reshape(seq, width)


def ring_pieces(block, axis):
    n = 4
    to_right = [(i, (i + 1) % n) for i in range(n)]
    to_left = [(i, (i - 1) % n) for i in range(n)]
    from_left = lax.ppermute(block, axis, to_right)
    from_right = lax.ppermute(block, axis, to_left)
    half = block.shape[1] // 2
    far_low = lax.ppermute(from_left[:, :half], axis, to_right)
    far_high = lax.ppermute(from_right[:, half:], axis, to_left)
    return block, from_right, far_low, far_high, from_left


def near_kernel(a_ref, w0_ref, w1_ref, w3_ref, *o_refs):
    k = w0_ref.shape[0]
    quarter = o_refs[0].shape[1]
    a = a_ref[...]
    base = jnp.dot(a[:, 0:k], w0_ref[...], preferred_element_type=jnp.float32)
    base = base + jnp.dot(a[:, k:2 * k], w1_ref[...], preferred_element_type=jnp.float32)
    base = base + jnp.dot(a[:, 3 * k:4 * k], w3_ref[...], preferred_element_type=jnp.float32)
    for q, o_ref in enumerate(o_refs):
        o_ref[...] = base[:, q * quarter:(q + 1) * quarter]


def far_kernel(a_ref, w2lo_ref, w2hi_ref, *refs):
    k = w2lo_ref.shape[0]
    acc_refs, o_refs = refs[:4], refs[4:]
    quarter = o_refs[0].shape[1]
    far = a_ref[:, 2 * k:3 * k]
    low = jnp.dot(far, w2lo_ref[...], preferred_element_type=jnp.float32)
    high = jnp.dot(far, w2hi_ref[...], preferred_element_type=jnp.float32)
    for q, (acc_ref, o_ref) in enumerate(zip(acc_refs, o_refs)):
        source = low if q < 2 else high
        start = (q % 2) * quarter
        o_ref[...] = acc_ref[...] + source[:, start:start + quarter]


def dot_pieces(a, pieces, tile=256):
    m, kk = a.shape
    n = pieces[0].shape[1]
    own, right, far_low, far_high, left = pieces
    full = lambda p: pl.BlockSpec(p.shape, lambda i: (0, 0))
    spec = pl.BlockSpec((tile, n // 4), lambda i: (i, 0))
    shape = jax.ShapeDtypeStruct((m, n // 4), jnp.float32)
    a_spec = pl.BlockSpec((tile, kk), lambda i: (i, 0))
    near_w = (own, right, left)
    quarters = pl.pallas_call(
        near_kernel,
        grid=(m // tile,),
        in_specs=[a_spec] + [full(p) for p in near_w],
        out_specs=(spec,) * 4,
        out_shape=(shape,) * 4,
        cost_estimate=pl.CostEstimate(
            flops=2 * m * 3 * own.size, transcendentals=0, bytes_accessed=a.size * 2 + 3 * own.size * 2 + m * n * 4
        ),
    )(a, *near_w)
    return pl.pallas_call(
        far_kernel,
        grid=(m // tile,),
        in_specs=[a_spec, full(far_low), full(far_high)] + [spec] * 4,
        out_specs=(spec,) * 4,
        out_shape=(shape,) * 4,
        input_output_aliases={3: 0, 4: 1, 5: 2, 6: 3},
        cost_estimate=pl.CostEstimate(
            flops=2 * m * own.size, transcendentals=0, bytes_accessed=a.size * 2 + own.size * 2 + 2 * m * n * 4
        ),
    )(a, far_low, far_high, *quarters)


def ring_reduce_scatter(parts, axis, n):
    me = lax.axis_index(axis)
    out = []
    for index, part in enumerate(parts):
        step_dir = 1 if index % 2 == 0 else -1
        perm = [(i, (i + step_dir) % n) for i in range(n)]
        acc = lax.dynamic_index_in_dim(part, (me - step_dir) % n, 0, keepdims=False)
        for k in range(n - 1):
            got = lax.ppermute(acc, axis, perm)
            seg = (me - step_dir * (k + 2)) % n
            acc = got + lax.dynamic_index_in_dim(part, seg, 0, keepdims=False)
        out.append(acc)
    return jnp.concatenate(out, axis=1)


def per_device(q_seq, k_seq, v_seq, resid, ln_gain, w_up, n_x):
    pieces = ring_pieces(w_up, "rx")
    attended = attention_block(q_seq, k_seq, v_seq)
    both = jnp.stack([resid, attended], axis=1)
    both = lax.all_to_all(both, "col", split_axis=0, concat_axis=1, tiled=True)
    chunk = both.shape[0]
    both = both.reshape(chunk, -1, 2, resid.shape[1])
    stream = (both[:, :, 0].astype(jnp.float32) + both[:, :, 1].astype(jnp.float32)).reshape(chunk, -1)
    full_width = stream.shape[1]
    mean = jnp.sum(stream, axis=1, keepdims=True) / full_width
    spread = jnp.sum(stream * stream, axis=1, keepdims=True) / full_width - mean * mean
    normed = ((stream - mean) * lax.rsqrt(spread + 1e-05) * ln_gain[None, :]).astype(jnp.bfloat16)
    block = w_up.shape[0]
    n_y = full_width // (n_x * block)
    grouped = normed.reshape(chunk, n_y, n_x, block)
    doubled = jnp.concatenate([grouped, grouped], axis=2)
    rolled = lax.dynamic_slice_in_dim(doubled, lax.axis_index("rx"), n_x, axis=2).reshape(chunk, full_width)
    n_col = lax.axis_size("col")
    groups = rolled.reshape(chunk, n_y, -1).transpose(1, 0, 2)
    spread_out = jnp.broadcast_to(groups[:, None], (n_y, n_col) + groups.shape[1:])
    spread_out = spread_out.reshape((n_y * n_col,) + groups.shape[1:])
    tokens = lax.all_to_all(spread_out, ("ry", "col"), split_axis=0, concat_axis=0, tiled=True)
    tokens = tokens.reshape(-1, tokens.shape[-1])
    quarters = dot_pieces(tokens, pieces)
    product = ring_reduce_scatter([q.reshape(n_y, -1, q.shape[1]) for q in quarters], "ry", n_y)
    return jax.nn.gelu(product, approximate=True).astype(jnp.bfloat16)


def solution(mesh):
    n_row, n_col = mesh.shape["row"], mesh.shape["col"]
    nx = len({d.coords[0] for d in mesh.devices[:, 0]})
    split = Mesh(mesh.devices.reshape(n_row // nx, nx, n_col), ("ry", "rx", "col"))
    rows = ("ry", "rx")
    placed = (
        P(rows, "col"),
        P(rows, "col"),
        P(rows, "col"),
        P(rows, "col"),
        P(),
        P(rows, "col"),
    )

    def body(q_seq, k_seq, v_seq, resid, ln_gain, w_up):
        return per_device(q_seq, k_seq, v_seq, resid, ln_gain, w_up, nx)

    return jax.shard_map(body, mesh=split, in_specs=placed, out_specs=P(rows, "col"), check_vma=False)
```

```python
import math

import jax
import jax.numpy as jnp
from jax import lax
from jax.experimental import pallas as pl
from jax.sharding import Mesh, PartitionSpec as P

HD = 128


def attention_block(query, keys, values):
    seq, width = query.shape
    heads = width // HD
    qshaped = query.reshape(seq, heads, HD)
    kshaped = keys.reshape(seq, heads, HD)
    vshaped = values.reshape(seq, heads, HD)
    scores = jnp.einsum("qhd,khd->hqk", qshaped, kshaped, preferred_element_type=jnp.float32)
    scores = scores * (1.0 / math.sqrt(HD))
    rows_idx = lax.broadcasted_iota(jnp.int32, (seq, seq), 0)
    cols_idx = lax.broadcasted_iota(jnp.int32, (seq, seq), 1)
    scores = jnp.where((rows_idx >= cols_idx)[None], scores, -1e30)
    highest = jnp.max(scores, axis=-1, keepdims=True)
    expo = jnp.exp(scores - highest)
    prob = (expo / jnp.sum(expo, axis=-1, keepdims=True)).astype(jnp.bfloat16)
    output = jnp.einsum("hqk,khd->qhd", prob, vshaped, preferred_element_type=jnp.float32)
    return output.astype(jnp.bfloat16).reshape(seq, width)


def ring_pieces(block, axis):
    n = 4
    to_right = [(i, (i + 1) % n) for i in range(n)]
    to_left = [(i, (i - 1) % n) for i in range(n)]
    from_left = lax.ppermute(block, axis, to_right)
    from_right = lax.ppermute(block, axis, to_left)
    half = block.shape[1] // 2
    far_low = lax.ppermute(from_left[:, :half], axis, to_right)
    far_high = lax.ppermute(from_right[:, half:], axis, to_left)
    return block, from_right, far_low, far_high, from_left


def near_kernel(a_ref, w0_ref, w1_ref, w3_ref, *o_refs):
    k = w0_ref.shape[0]
    quarter = o_refs[0].shape[1]
    a = a_ref[...]
    base = jnp.dot(a[:, 0:k], w0_ref[...], preferred_element_type=jnp.float32)
    base = base + jnp.dot(a[:, k:2 * k], w1_ref[...], preferred_element_type=jnp.float32)
    base = base + jnp.dot(a[:, 3 * k:4 * k], w3_ref[...], preferred_element_type=jnp.float32)
    for q, o_ref in enumerate(o_refs):
        o_ref[...] = base[:, q * quarter:(q + 1) * quarter]


def far_kernel(a_ref, w2lo_ref, w2hi_ref, *o_refs):
    k = w2lo_ref.shape[0]
    quarter = o_refs[0].shape[1]
    far = a_ref[:, 2 * k:3 * k]
    low = jnp.dot(far, w2lo_ref[...], preferred_element_type=jnp.float32)
    high = jnp.dot(far, w2hi_ref[...], preferred_element_type=jnp.float32)
    for q, o_ref in enumerate(o_refs):
        source = low if q < 2 else high
        start = (q % 2) * quarter
        o_ref[...] = source[:, start:start + quarter]


def dot_pieces(a, pieces, tile=256):
    m, kk = a.shape
    n = pieces[0].shape[1]
    own, right, far_low, far_high, left = pieces
    full = lambda p: pl.BlockSpec(p.shape, lambda i: (0, 0))
    spec = pl.BlockSpec((tile, n // 4), lambda i: (i, 0))
    shape = jax.ShapeDtypeStruct((m, n // 4), jnp.float32)
    a_spec = pl.BlockSpec((tile, kk), lambda i: (i, 0))
    near_w = (own, right, left)
    quarters = pl.pallas_call(
        near_kernel,
        grid=(m // tile,),
        in_specs=[a_spec] + [full(p) for p in near_w],
        out_specs=(spec,) * 4,
        out_shape=(shape,) * 4,
        cost_estimate=pl.CostEstimate(
            flops=2 * m * 3 * own.size, transcendentals=0, bytes_accessed=a.size * 2 + 3 * own.size * 2 + m * n * 4
        ),
    )(a, *near_w)
    far_quarters = pl.pallas_call(
        far_kernel,
        grid=(m // tile,),
        in_specs=[a_spec, full(far_low), full(far_high)],
        out_specs=(spec,) * 4,
        out_shape=(shape,) * 4,
        cost_estimate=pl.CostEstimate(
            flops=2 * m * own.size, transcendentals=0, bytes_accessed=a.size * 2 + own.size * 2 + m * n * 4
        ),
    )(a, far_low, far_high)
    return quarters, far_quarters


def ring_reduce_scatter(parts, others, axis, n, finish):
    me = lax.axis_index(axis)
    out = []
    for index, (part, other) in enumerate(zip(parts, others)):
        step_dir = 1 if index % 2 == 0 else -1
        perm = [(i, (i + step_dir) % n) for i in range(n)]
        own = lambda seg: lax.dynamic_index_in_dim(part, seg, 0, keepdims=False) + lax.dynamic_index_in_dim(
            other, seg, 0, keepdims=False
        )
        acc = own((me - step_dir) % n)
        for k in range(n - 1):
            got = lax.ppermute(acc, axis, perm)
            acc = got + own((me - step_dir * (k + 2)) % n)
        out.append(finish(acc))
    return jnp.concatenate(out, axis=1)


def per_device(q_seq, k_seq, v_seq, resid, ln_gain, w_up, n_x):
    pieces = ring_pieces(w_up, "rx")
    attended = attention_block(q_seq, k_seq, v_seq)
    both = jnp.stack([resid, attended], axis=1)
    both = lax.all_to_all(both, "col", split_axis=0, concat_axis=1, tiled=True)
    chunk = both.shape[0]
    both = both.reshape(chunk, -1, 2, resid.shape[1])
    stream = (both[:, :, 0].astype(jnp.float32) + both[:, :, 1].astype(jnp.float32)).reshape(chunk, -1)
    full_width = stream.shape[1]
    mean = jnp.sum(stream, axis=1, keepdims=True) / full_width
    spread = jnp.sum(stream * stream, axis=1, keepdims=True) / full_width - mean * mean
    normed = ((stream - mean) * lax.rsqrt(spread + 1e-05) * ln_gain[None, :]).astype(jnp.bfloat16)
    block = w_up.shape[0]
    n_y = full_width // (n_x * block)
    grouped = normed.reshape(chunk, n_y, n_x, block)
    doubled = jnp.concatenate([grouped, grouped], axis=2)
    rolled = lax.dynamic_slice_in_dim(doubled, lax.axis_index("rx"), n_x, axis=2).reshape(chunk, full_width)
    n_col = lax.axis_size("col")
    groups = rolled.reshape(chunk, n_y, -1).transpose(1, 0, 2)
    spread_out = jnp.broadcast_to(groups[:, None], (n_y, n_col) + groups.shape[1:])
    spread_out = spread_out.reshape((n_y * n_col,) + groups.shape[1:])
    tokens = lax.all_to_all(spread_out, ("ry", "col"), split_axis=0, concat_axis=0, tiled=True)
    tokens = tokens.reshape(-1, tokens.shape[-1])
    near, far = dot_pieces(tokens, pieces)
    segments = lambda qs: [q.reshape(n_y, -1, q.shape[1]) for q in qs]
    finish = lambda u: jax.nn.gelu(u, approximate=True).astype(jnp.bfloat16)
    return ring_reduce_scatter(segments(near), segments(far), "ry", n_y, finish)


def solution(mesh):
    n_row, n_col = mesh.shape["row"], mesh.shape["col"]
    nx = len({d.coords[0] for d in mesh.devices[:, 0]})
    split = Mesh(mesh.devices.reshape(n_row // nx, nx, n_col), ("ry", "rx", "col"))
    rows = ("ry", "rx")
    placed = (
        P(rows, "col"),
        P(rows, "col"),
        P(rows, "col"),
        P(rows, "col"),
        P(),
        P(rows, "col"),
    )

    def body(q_seq, k_seq, v_seq, resid, ln_gain, w_up):
        return per_device(q_seq, k_seq, v_seq, resid, ln_gain, w_up, nx)

    return jax.shard_map(body, mesh=split, in_specs=placed, out_specs=P(rows, "col"), check_vma=False)
```

```python
import math

import jax
import jax.numpy as jnp
from jax import lax
from jax.experimental import pallas as pl
from jax.sharding import Mesh, PartitionSpec as P

HD = 128


def attention_block(query, keys, values):
    seq, width = query.shape
    heads = width // HD
    qshaped = query.reshape(seq, heads, HD)
    kshaped = keys.reshape(seq, heads, HD)
    vshaped = values.reshape(seq, heads, HD)
    scores = jnp.einsum("qhd,khd->hqk", qshaped, kshaped, preferred_element_type=jnp.float32)
    scores = scores * (1.0 / math.sqrt(HD))
    rows_idx = lax.broadcasted_iota(jnp.int32, (seq, seq), 0)
    cols_idx = lax.broadcasted_iota(jnp.int32, (seq, seq), 1)
    scores = jnp.where((rows_idx >= cols_idx)[None], scores, -1e30)
    highest = jnp.max(scores, axis=-1, keepdims=True)
    expo = jnp.exp(scores - highest)
    prob = (expo / jnp.sum(expo, axis=-1, keepdims=True)).astype(jnp.bfloat16)
    output = jnp.einsum("hqk,khd->qhd", prob, vshaped, preferred_element_type=jnp.float32)
    return output.astype(jnp.bfloat16).reshape(seq, width)


def ring_pieces(block, axis):
    n = 4
    to_right = [(i, (i + 1) % n) for i in range(n)]
    to_left = [(i, (i - 1) % n) for i in range(n)]
    from_left = lax.ppermute(block, axis, to_right)
    from_right = lax.ppermute(block, axis, to_left)
    half = block.shape[1] // 2
    far_low = lax.ppermute(from_left[:, :half], axis, to_right)
    far_high = lax.ppermute(from_right[:, half:], axis, to_left)
    return block, from_right, far_low, far_high, from_left


def near_kernel(a_ref, w0_ref, w1_ref, w3_ref, *o_refs):
    k = w0_ref.shape[0]
    quarter = o_refs[0].shape[1]
    a = a_ref[...]
    base = jnp.dot(a[:, 0:k], w0_ref[...], preferred_element_type=jnp.float32)
    base = base + jnp.dot(a[:, k:2 * k], w1_ref[...], preferred_element_type=jnp.float32)
    base = base + jnp.dot(a[:, 3 * k:4 * k], w3_ref[...], preferred_element_type=jnp.float32)
    for q, o_ref in enumerate(o_refs):
        o_ref[...] = base[:, q * quarter:(q + 1) * quarter]


def far_kernel(a_ref, w2lo_ref, w2hi_ref, *o_refs):
    k = w2lo_ref.shape[0]
    quarter = o_refs[0].shape[1]
    far = a_ref[:, 2 * k:3 * k]
    low = jnp.dot(far, w2lo_ref[...], preferred_element_type=jnp.float32)
    high = jnp.dot(far, w2hi_ref[...], preferred_element_type=jnp.float32)
    for q, o_ref in enumerate(o_refs):
        source = low if q < 2 else high
        start = (q % 2) * quarter
        o_ref[...] = source[:, start:start + quarter]


def dot_pieces(a, pieces, tile=512):
    m, kk = a.shape
    n = pieces[0].shape[1]
    own, right, far_low, far_high, left = pieces
    full = lambda p: pl.BlockSpec(p.shape, lambda i: (0, 0))
    spec = pl.BlockSpec((tile, n // 4), lambda i: (i, 0))
    shape = jax.ShapeDtypeStruct((m, n // 4), jnp.float32)
    a_spec = pl.BlockSpec((tile, kk), lambda i: (i, 0))
    near_w = (own, right, left)
    quarters = pl.pallas_call(
        near_kernel,
        grid=(m // tile,),
        in_specs=[a_spec] + [full(p) for p in near_w],
        out_specs=(spec,) * 4,
        out_shape=(shape,) * 4,
        cost_estimate=pl.CostEstimate(
            flops=2 * m * 3 * own.size, transcendentals=0, bytes_accessed=a.size * 2 + 3 * own.size * 2 + m * n * 4
        ),
    )(a, *near_w)
    far_quarters = pl.pallas_call(
        far_kernel,
        grid=(m // tile,),
        in_specs=[a_spec, full(far_low), full(far_high)],
        out_specs=(spec,) * 4,
        out_shape=(shape,) * 4,
        cost_estimate=pl.CostEstimate(
            flops=2 * m * own.size, transcendentals=0, bytes_accessed=a.size * 2 + own.size * 2 + m * n * 4
        ),
    )(a, far_low, far_high)
    return quarters, far_quarters


def ring_reduce_scatter(parts, others, axis, n, finish):
    me = lax.axis_index(axis)
    out = []
    for index, (part, other) in enumerate(zip(parts, others)):
        step_dir = 1 if index % 2 == 0 else -1
        perm = [(i, (i + step_dir) % n) for i in range(n)]
        own = lambda seg: lax.dynamic_index_in_dim(part, seg, 0, keepdims=False) + lax.dynamic_index_in_dim(
            other, seg, 0, keepdims=False
        )
        acc = own((me - step_dir) % n)
        for k in range(n - 1):
            got = lax.ppermute(acc, axis, perm)
            acc = got + own((me - step_dir * (k + 2)) % n)
        out.append(finish(acc))
    return jnp.concatenate(out, axis=1)


def per_device(q_seq, k_seq, v_seq, resid, ln_gain, w_up, n_x):
    pieces = ring_pieces(w_up, "rx")
    attended = attention_block(q_seq, k_seq, v_seq)
    both = jnp.stack([resid, attended], axis=1)
    both = lax.all_to_all(both, "col", split_axis=0, concat_axis=1, tiled=True)
    chunk = both.shape[0]
    both = both.reshape(chunk, -1, 2, resid.shape[1])
    stream = (both[:, :, 0].astype(jnp.float32) + both[:, :, 1].astype(jnp.float32)).reshape(chunk, -1)
    full_width = stream.shape[1]
    mean = jnp.sum(stream, axis=1, keepdims=True) / full_width
    spread = jnp.sum(stream * stream, axis=1, keepdims=True) / full_width - mean * mean
    normed = ((stream - mean) * lax.rsqrt(spread + 1e-05) * ln_gain[None, :]).astype(jnp.bfloat16)
    block = w_up.shape[0]
    n_y = full_width // (n_x * block)
    grouped = normed.reshape(chunk, n_y, n_x, block)
    doubled = jnp.concatenate([grouped, grouped], axis=2)
    rolled = lax.dynamic_slice_in_dim(doubled, lax.axis_index("rx"), n_x, axis=2).reshape(chunk, full_width)
    n_col = lax.axis_size("col")
    groups = rolled.reshape(chunk, n_y, -1).transpose(1, 0, 2)
    spread_out = jnp.broadcast_to(groups[:, None], (n_y, n_col) + groups.shape[1:])
    spread_out = spread_out.reshape((n_y * n_col,) + groups.shape[1:])
    tokens = lax.all_to_all(spread_out, ("ry", "col"), split_axis=0, concat_axis=0, tiled=True)
    tokens = tokens.reshape(-1, tokens.shape[-1])
    near, far = dot_pieces(tokens, pieces)
    segments = lambda qs: [q.reshape(n_y, -1, q.shape[1]) for q in qs]
    finish = lambda u: jax.nn.gelu(u, approximate=True).astype(jnp.bfloat16)
    return ring_reduce_scatter(segments(near), segments(far), "ry", n_y, finish)


def solution(mesh):
    n_row, n_col = mesh.shape["row"], mesh.shape["col"]
    nx = len({d.coords[0] for d in mesh.devices[:, 0]})
    split = Mesh(mesh.devices.reshape(n_row // nx, nx, n_col), ("ry", "rx", "col"))
    rows = ("ry", "rx")
    placed = (
        P(rows, "col"),
        P(rows, "col"),
        P(rows, "col"),
        P(rows, "col"),
        P(),
        P(rows, "col"),
    )

    def body(q_seq, k_seq, v_seq, resid, ln_gain, w_up):
        return per_device(q_seq, k_seq, v_seq, resid, ln_gain, w_up, nx)

    return jax.shard_map(body, mesh=split, in_specs=placed, out_specs=P(rows, "col"), check_vma=False)
```

```python
import math

import jax
import jax.numpy as jnp
from jax import lax
from jax.experimental import pallas as pl
from jax.sharding import Mesh, PartitionSpec as P

HD = 128


def attention_block(query, keys, values):
    seq, width = query.shape
    heads = width // HD
    qshaped = query.reshape(seq, heads, HD)
    kshaped = keys.reshape(seq, heads, HD)
    vshaped = values.reshape(seq, heads, HD)
    scores = jnp.einsum("qhd,khd->hqk", qshaped, kshaped, preferred_element_type=jnp.float32)
    scores = scores * (1.0 / math.sqrt(HD))
    rows_idx = lax.broadcasted_iota(jnp.int32, (seq, seq), 0)
    cols_idx = lax.broadcasted_iota(jnp.int32, (seq, seq), 1)
    scores = jnp.where((rows_idx >= cols_idx)[None], scores, -1e30)
    highest = jnp.max(scores, axis=-1, keepdims=True)
    expo = jnp.exp(scores - highest)
    prob = (expo / jnp.sum(expo, axis=-1, keepdims=True)).astype(jnp.bfloat16)
    output = jnp.einsum("hqk,khd->qhd", prob, vshaped, preferred_element_type=jnp.float32)
    return output.astype(jnp.bfloat16).reshape(seq, width)


def ring_pieces(block, axis):
    n = 4
    to_right = [(i, (i + 1) % n) for i in range(n)]
    to_left = [(i, (i - 1) % n) for i in range(n)]
    from_left = lax.ppermute(block, axis, to_right)
    from_right = lax.ppermute(block, axis, to_left)
    half = block.shape[1] // 2
    far_low = lax.ppermute(from_left[:, :half], axis, to_right)
    far_high = lax.ppermute(from_right[:, half:], axis, to_left)
    return block, from_right, far_low, far_high, from_left


def near_kernel(a_ref, w0_ref, w1_ref, w3_ref, *o_refs):
    k = w0_ref.shape[0]
    quarter = o_refs[0].shape[1]
    a = a_ref[...]
    base = jnp.dot(a[:, 0:k], w0_ref[...], preferred_element_type=jnp.float32)
    base = base + jnp.dot(a[:, k:2 * k], w1_ref[...], preferred_element_type=jnp.float32)
    base = base + jnp.dot(a[:, 3 * k:4 * k], w3_ref[...], preferred_element_type=jnp.float32)
    for q, o_ref in enumerate(o_refs):
        o_ref[...] = base[:, q * quarter:(q + 1) * quarter]


def far_kernel(a_ref, w2lo_ref, w2hi_ref, *o_refs):
    k = w2lo_ref.shape[0]
    quarter = o_refs[0].shape[1]
    far = a_ref[:, 2 * k:3 * k]
    low = jnp.dot(far, w2lo_ref[...], preferred_element_type=jnp.float32)
    high = jnp.dot(far, w2hi_ref[...], preferred_element_type=jnp.float32)
    for q, o_ref in enumerate(o_refs):
        source = low if q < 2 else high
        start = (q % 2) * quarter
        o_ref[...] = source[:, start:start + quarter]


def dot_pieces(a, pieces, tile=256):
    m, kk = a.shape
    n = pieces[0].shape[1]
    own, right, far_low, far_high, left = pieces
    full = lambda p: pl.BlockSpec(p.shape, lambda i: (0, 0))
    spec = pl.BlockSpec((tile, n // 4), lambda i: (i, 0))
    shape = jax.ShapeDtypeStruct((m, n // 4), jnp.float32)
    a_spec = pl.BlockSpec((tile, kk), lambda i: (i, 0))
    near_w = (own, right, left)
    quarters = pl.pallas_call(
        near_kernel,
        grid=(m // tile,),
        in_specs=[a_spec] + [full(p) for p in near_w],
        out_specs=(spec,) * 4,
        out_shape=(shape,) * 4,
        cost_estimate=pl.CostEstimate(
            flops=2 * m * 3 * own.size, transcendentals=0, bytes_accessed=a.size * 2 + 3 * own.size * 2 + m * n * 4
        ),
    )(a, *near_w)
    far_quarters = pl.pallas_call(
        far_kernel,
        grid=(m // tile,),
        in_specs=[a_spec, full(far_low), full(far_high)],
        out_specs=(spec,) * 4,
        out_shape=(shape,) * 4,
        cost_estimate=pl.CostEstimate(
            flops=2 * m * own.size, transcendentals=0, bytes_accessed=a.size * 2 + own.size * 2 + m * n * 4
        ),
    )(a, far_low, far_high)
    return quarters, far_quarters


def ring_reduce_scatter(parts, others, axis, n, finish):
    me = lax.axis_index(axis)
    out = []
    for index, (part, other) in enumerate(zip(parts, others)):
        step_dir = 1 if index % 2 == 0 else -1
        perm = [(i, (i + step_dir) % n) for i in range(n)]
        own = lambda seg: lax.dynamic_index_in_dim(part, seg, 0, keepdims=False) + lax.dynamic_index_in_dim(
            other, seg, 0, keepdims=False
        )
        acc = own((me - step_dir) % n)
        for k in range(n - 1):
            got = lax.ppermute(acc, axis, perm)
            acc = got + own((me - step_dir * (k + 2)) % n)
        out.append(finish(acc))
    return jnp.concatenate(out, axis=1)


def per_device(q_seq, k_seq, v_seq, resid, ln_gain, w_up, n_x):
    pieces = ring_pieces(w_up, "rx")
    attended = attention_block(q_seq, k_seq, v_seq)
    both = jnp.concatenate([resid, attended], axis=1)
    both = lax.all_to_all(both, "col", split_axis=0, concat_axis=1, tiled=True)
    chunk = both.shape[0]
    both = both.reshape(chunk, -1, 2, resid.shape[1])
    stream = (both[:, :, 0].astype(jnp.float32) + both[:, :, 1].astype(jnp.float32)).reshape(chunk, -1)
    full_width = stream.shape[1]
    mean = jnp.sum(stream, axis=1, keepdims=True) / full_width
    spread = jnp.sum(stream * stream, axis=1, keepdims=True) / full_width - mean * mean
    normed = ((stream - mean) * lax.rsqrt(spread + 1e-05) * ln_gain[None, :]).astype(jnp.bfloat16)
    block = w_up.shape[0]
    n_y = full_width // (n_x * block)
    grouped = normed.reshape(chunk, n_y, n_x, block)
    doubled = jnp.concatenate([grouped, grouped], axis=2)
    rolled = lax.dynamic_slice_in_dim(doubled, lax.axis_index("rx"), n_x, axis=2).reshape(chunk, full_width)
    n_col = lax.axis_size("col")
    groups = rolled.reshape(chunk, n_y, -1).transpose(1, 0, 2)
    spread_out = jnp.broadcast_to(groups[:, None], (n_y, n_col) + groups.shape[1:])
    spread_out = spread_out.reshape((n_y * n_col,) + groups.shape[1:])
    tokens = lax.all_to_all(spread_out, ("ry", "col"), split_axis=0, concat_axis=0, tiled=True)
    tokens = tokens.reshape(-1, tokens.shape[-1])
    near, far = dot_pieces(tokens, pieces)
    segments = lambda qs: [q.reshape(n_y, -1, q.shape[1]) for q in qs]
    finish = lambda u: jax.nn.gelu(u, approximate=True).astype(jnp.bfloat16)
    return ring_reduce_scatter(segments(near), segments(far), "ry", n_y, finish)


def solution(mesh):
    n_row, n_col = mesh.shape["row"], mesh.shape["col"]
    nx = len({d.coords[0] for d in mesh.devices[:, 0]})
    split = Mesh(mesh.devices.reshape(n_row // nx, nx, n_col), ("ry", "rx", "col"))
    rows = ("ry", "rx")
    placed = (
        P(rows, "col"),
        P(rows, "col"),
        P(rows, "col"),
        P(rows, "col"),
        P(),
        P(rows, "col"),
    )

    def body(q_seq, k_seq, v_seq, resid, ln_gain, w_up):
        return per_device(q_seq, k_seq, v_seq, resid, ln_gain, w_up, nx)

    return jax.shard_map(body, mesh=split, in_specs=placed, out_specs=P(rows, "col"), check_vma=False)
```

```python
import math

import jax
import jax.numpy as jnp
from jax import lax
from jax.experimental import pallas as pl
from jax.sharding import Mesh, PartitionSpec as P

HD = 128


def attention_block(query, keys, values):
    seq, width = query.shape
    heads = width // HD
    qshaped = query.reshape(seq, heads, HD)
    kshaped = keys.reshape(seq, heads, HD)
    vshaped = values.reshape(seq, heads, HD)
    scores = jnp.einsum("qhd,khd->hqk", qshaped, kshaped, preferred_element_type=jnp.float32)
    scores = scores * (1.0 / math.sqrt(HD))
    rows_idx = lax.broadcasted_iota(jnp.int32, (seq, seq), 0)
    cols_idx = lax.broadcasted_iota(jnp.int32, (seq, seq), 1)
    scores = jnp.where((rows_idx >= cols_idx)[None], scores, -1e30)
    highest = jnp.max(scores, axis=-1, keepdims=True)
    expo = jnp.exp(scores - highest)
    prob = (expo / jnp.sum(expo, axis=-1, keepdims=True)).astype(jnp.bfloat16)
    output = jnp.einsum("hqk,khd->qhd", prob, vshaped, preferred_element_type=jnp.float32)
    return output.astype(jnp.bfloat16).reshape(seq, width)


def ring_pieces(block, axis):
    n = 4
    to_right = [(i, (i + 1) % n) for i in range(n)]
    to_left = [(i, (i - 1) % n) for i in range(n)]
    from_left = lax.ppermute(block, axis, to_right)
    from_right = lax.ppermute(block, axis, to_left)
    half = block.shape[1] // 2
    far_low = lax.ppermute(from_left[:, :half], axis, to_right)
    far_high = lax.ppermute(from_right[:, half:], axis, to_left)
    return block, from_right, far_low, far_high, from_left


def near_kernel(a_ref, w0_ref, w1_ref, w3_ref, *o_refs):
    k = w0_ref.shape[0]
    quarter = o_refs[0].shape[1]
    a = a_ref[...]
    base = jnp.dot(a[:, 0:k], w0_ref[...], preferred_element_type=jnp.float32)
    base = base + jnp.dot(a[:, k:2 * k], w1_ref[...], preferred_element_type=jnp.float32)
    base = base + jnp.dot(a[:, 3 * k:4 * k], w3_ref[...], preferred_element_type=jnp.float32)
    for q, o_ref in enumerate(o_refs):
        o_ref[...] = base[:, q * quarter:(q + 1) * quarter]


def far_kernel(a_ref, w2_ref, *o_refs):
    k = w2_ref.shape[0]
    quarter = o_refs[0].shape[1]
    product = jnp.dot(a_ref[:, 2 * k:3 * k], w2_ref[...], preferred_element_type=jnp.float32)
    for q, o_ref in enumerate(o_refs):
        o_ref[...] = product[:, q * quarter:(q + 1) * quarter]


def dot_pieces(a, pieces, tile=256):
    m, kk = a.shape
    n = pieces[0].shape[1]
    own, right, far_low, far_high, left = pieces
    full = lambda p: pl.BlockSpec(p.shape, lambda i: (0, 0))
    spec = pl.BlockSpec((tile, n // 4), lambda i: (i, 0))
    shape = jax.ShapeDtypeStruct((m, n // 4), jnp.float32)
    a_spec = pl.BlockSpec((tile, kk), lambda i: (i, 0))
    near_w = (own, right, left)
    quarters = pl.pallas_call(
        near_kernel,
        grid=(m // tile,),
        in_specs=[a_spec] + [full(p) for p in near_w],
        out_specs=(spec,) * 4,
        out_shape=(shape,) * 4,
        cost_estimate=pl.CostEstimate(
            flops=2 * m * 3 * own.size, transcendentals=0, bytes_accessed=a.size * 2 + 3 * own.size * 2 + m * n * 4
        ),
    )(a, *near_w)
    far_quarters = ()
    for far_half in (far_low, far_high):
        far_quarters += pl.pallas_call(
            far_kernel,
            grid=(m // tile,),
            in_specs=[a_spec, full(far_half)],
            out_specs=(spec,) * 2,
            out_shape=(shape,) * 2,
            cost_estimate=pl.CostEstimate(
                flops=2 * m * far_half.size, transcendentals=0, bytes_accessed=a.size * 2 + far_half.size * 2 + m * n * 2
            ),
        )(a, far_half)
    return quarters, far_quarters


def ring_reduce_scatter(parts, others, axis, n, finish):
    me = lax.axis_index(axis)
    out = []
    for index, (part, other) in enumerate(zip(parts, others)):
        step_dir = 1 if index % 2 == 0 else -1
        perm = [(i, (i + step_dir) % n) for i in range(n)]
        own = lambda seg: lax.dynamic_index_in_dim(part, seg, 0, keepdims=False) + lax.dynamic_index_in_dim(
            other, seg, 0, keepdims=False
        )
        acc = own((me - step_dir) % n)
        for k in range(n - 1):
            got = lax.ppermute(acc, axis, perm)
            acc = got + own((me - step_dir * (k + 2)) % n)
        out.append(finish(acc))
    return jnp.concatenate(out, axis=1)


def per_device(q_seq, k_seq, v_seq, resid, ln_gain, w_up, n_x):
    pieces = ring_pieces(w_up, "rx")
    attended = attention_block(q_seq, k_seq, v_seq)
    both = jnp.concatenate([resid, attended], axis=1)
    both = lax.all_to_all(both, "col", split_axis=0, concat_axis=1, tiled=True)
    chunk = both.shape[0]
    both = both.reshape(chunk, -1, 2, resid.shape[1])
    stream = (both[:, :, 0].astype(jnp.float32) + both[:, :, 1].astype(jnp.float32)).reshape(chunk, -1)
    full_width = stream.shape[1]
    mean = jnp.sum(stream, axis=1, keepdims=True) / full_width
    spread = jnp.sum(stream * stream, axis=1, keepdims=True) / full_width - mean * mean
    normed = ((stream - mean) * lax.rsqrt(spread + 1e-05) * ln_gain[None, :]).astype(jnp.bfloat16)
    block = w_up.shape[0]
    n_y = full_width // (n_x * block)
    grouped = normed.reshape(chunk, n_y, n_x, block)
    doubled = jnp.concatenate([grouped, grouped], axis=2)
    rolled = lax.dynamic_slice_in_dim(doubled, lax.axis_index("rx"), n_x, axis=2).reshape(chunk, full_width)
    n_col = lax.axis_size("col")
    groups = rolled.reshape(chunk, n_y, -1).transpose(1, 0, 2)
    spread_out = jnp.broadcast_to(groups[:, None], (n_y, n_col) + groups.shape[1:])
    spread_out = spread_out.reshape((n_y * n_col,) + groups.shape[1:])
    tokens = lax.all_to_all(spread_out, ("ry", "col"), split_axis=0, concat_axis=0, tiled=True)
    tokens = tokens.reshape(-1, tokens.shape[-1])
    near, far = dot_pieces(tokens, pieces)
    segments = lambda qs: [q.reshape(n_y, -1, q.shape[1]) for q in qs]
    finish = lambda u: jax.nn.gelu(u, approximate=True).astype(jnp.bfloat16)
    return ring_reduce_scatter(segments(near), segments(far), "ry", n_y, finish)


def solution(mesh):
    n_row, n_col = mesh.shape["row"], mesh.shape["col"]
    nx = len({d.coords[0] for d in mesh.devices[:, 0]})
    split = Mesh(mesh.devices.reshape(n_row // nx, nx, n_col), ("ry", "rx", "col"))
    rows = ("ry", "rx")
    placed = (
        P(rows, "col"),
        P(rows, "col"),
        P(rows, "col"),
        P(rows, "col"),
        P(),
        P(rows, "col"),
    )

    def body(q_seq, k_seq, v_seq, resid, ln_gain, w_up):
        return per_device(q_seq, k_seq, v_seq, resid, ln_gain, w_up, nx)

    return jax.shard_map(body, mesh=split, in_specs=placed, out_specs=P(rows, "col"), check_vma=False)
```

```python
import math

import jax
import jax.numpy as jnp
from jax import lax
from jax.experimental import pallas as pl
from jax.experimental.pallas import tpu as pltpu
from jax.sharding import Mesh, PartitionSpec as P

HD = 128


def attention_block(query, keys, values):
    seq, width = query.shape
    heads = width // HD
    qshaped = query.reshape(seq, heads, HD)
    kshaped = keys.reshape(seq, heads, HD)
    vshaped = values.reshape(seq, heads, HD)
    scores = jnp.einsum("qhd,khd->hqk", qshaped, kshaped, preferred_element_type=jnp.float32)
    scores = scores * (1.0 / math.sqrt(HD))
    rows_idx = lax.broadcasted_iota(jnp.int32, (seq, seq), 0)
    cols_idx = lax.broadcasted_iota(jnp.int32, (seq, seq), 1)
    scores = jnp.where((rows_idx >= cols_idx)[None], scores, -1e30)
    highest = jnp.max(scores, axis=-1, keepdims=True)
    expo = jnp.exp(scores - highest)
    prob = (expo / jnp.sum(expo, axis=-1, keepdims=True)).astype(jnp.bfloat16)
    output = jnp.einsum("hqk,khd->qhd", prob, vshaped, preferred_element_type=jnp.float32)
    return output.astype(jnp.bfloat16).reshape(seq, width)


def ring_pieces(block, axis):
    n = 4
    to_right = [(i, (i + 1) % n) for i in range(n)]
    to_left = [(i, (i - 1) % n) for i in range(n)]
    from_left = lax.ppermute(block, axis, to_right)
    from_right = lax.ppermute(block, axis, to_left)
    half = block.shape[1] // 2
    far_low = lax.ppermute(from_left[:, :half], axis, to_right)
    far_high = lax.ppermute(from_right[:, half:], axis, to_left)
    return block, from_right, far_low, far_high, from_left


def near_kernel(a_ref, w0_ref, w1_ref, w3_ref, *o_refs):
    k = w0_ref.shape[0]
    quarter = o_refs[0].shape[1]
    rows = o_refs[0].shape[0]
    a = a_ref[pl.ds(pl.multiple_of(pl.program_id(0) * rows, rows), rows), :]
    base = jnp.dot(a[:, 0:k], w0_ref[...], preferred_element_type=jnp.float32)
    base = base + jnp.dot(a[:, k:2 * k], w1_ref[...], preferred_element_type=jnp.float32)
    base = base + jnp.dot(a[:, 3 * k:4 * k], w3_ref[...], preferred_element_type=jnp.float32)
    for q, o_ref in enumerate(o_refs):
        o_ref[...] = base[:, q * quarter:(q + 1) * quarter]


def far_kernel(a_ref, w2lo_ref, w2hi_ref, *o_refs):
    k = w2lo_ref.shape[0]
    quarter = o_refs[0].shape[1]
    rows = o_refs[0].shape[0]
    far = a_ref[pl.ds(pl.multiple_of(pl.program_id(0) * rows, rows), rows), 2 * k:3 * k]
    low = jnp.dot(far, w2lo_ref[...], preferred_element_type=jnp.float32)
    high = jnp.dot(far, w2hi_ref[...], preferred_element_type=jnp.float32)
    for q, o_ref in enumerate(o_refs):
        source = low if q < 2 else high
        start = (q % 2) * quarter
        o_ref[...] = source[:, start:start + quarter]


def dot_pieces(a, pieces, tile=256):
    m, kk = a.shape
    n = pieces[0].shape[1]
    own, right, far_low, far_high, left = pieces
    full = lambda p: pl.BlockSpec(p.shape, lambda i: (0, 0))
    spec = pl.BlockSpec((tile, n // 4), lambda i: (i, 0))
    shape = jax.ShapeDtypeStruct((m, n // 4), jnp.float32)
    a_spec = pl.BlockSpec(memory_space=pltpu.VMEM)
    near_w = (own, right, left)
    quarters = pl.pallas_call(
        near_kernel,
        grid=(m // tile,),
        in_specs=[a_spec] + [full(p) for p in near_w],
        out_specs=(spec,) * 4,
        out_shape=(shape,) * 4,
        cost_estimate=pl.CostEstimate(
            flops=2 * m * 3 * own.size, transcendentals=0, bytes_accessed=a.size * 2 + 3 * own.size * 2 + m * n * 4
        ),
    )(a, *near_w)
    far_quarters = pl.pallas_call(
        far_kernel,
        grid=(m // tile,),
        in_specs=[a_spec, full(far_low), full(far_high)],
        out_specs=(spec,) * 4,
        out_shape=(shape,) * 4,
        cost_estimate=pl.CostEstimate(
            flops=2 * m * own.size, transcendentals=0, bytes_accessed=a.size * 2 + own.size * 2 + m * n * 4
        ),
    )(a, far_low, far_high)
    return quarters, far_quarters


def ring_reduce_scatter(parts, others, axis, n, finish):
    me = lax.axis_index(axis)
    out = []
    for index, (part, other) in enumerate(zip(parts, others)):
        step_dir = 1 if index % 2 == 0 else -1
        perm = [(i, (i + step_dir) % n) for i in range(n)]
        own = lambda seg: lax.dynamic_index_in_dim(part, seg, 0, keepdims=False) + lax.dynamic_index_in_dim(
            other, seg, 0, keepdims=False
        )
        acc = own((me - step_dir) % n)
        for k in range(n - 1):
            got = lax.ppermute(acc, axis, perm)
            acc = got + own((me - step_dir * (k + 2)) % n)
        out.append(finish(acc))
    return jnp.concatenate(out, axis=1)


def per_device(q_seq, k_seq, v_seq, resid, ln_gain, w_up, n_x):
    pieces = ring_pieces(w_up, "rx")
    attended = attention_block(q_seq, k_seq, v_seq)
    both = jnp.concatenate([resid, attended], axis=1)
    both = lax.all_to_all(both, "col", split_axis=0, concat_axis=1, tiled=True)
    chunk = both.shape[0]
    both = both.reshape(chunk, -1, 2, resid.shape[1])
    stream = (both[:, :, 0].astype(jnp.float32) + both[:, :, 1].astype(jnp.float32)).reshape(chunk, -1)
    full_width = stream.shape[1]
    mean = jnp.sum(stream, axis=1, keepdims=True) / full_width
    spread = jnp.sum(stream * stream, axis=1, keepdims=True) / full_width - mean * mean
    normed = ((stream - mean) * lax.rsqrt(spread + 1e-05) * ln_gain[None, :]).astype(jnp.bfloat16)
    block = w_up.shape[0]
    n_y = full_width // (n_x * block)
    grouped = normed.reshape(chunk, n_y, n_x, block)
    doubled = jnp.concatenate([grouped, grouped], axis=2)
    rolled = lax.dynamic_slice_in_dim(doubled, lax.axis_index("rx"), n_x, axis=2).reshape(chunk, full_width)
    n_col = lax.axis_size("col")
    groups = rolled.reshape(chunk, n_y, -1).transpose(1, 0, 2)
    spread_out = jnp.broadcast_to(groups[:, None], (n_y, n_col) + groups.shape[1:])
    spread_out = spread_out.reshape((n_y * n_col,) + groups.shape[1:])
    tokens = lax.all_to_all(spread_out, ("ry", "col"), split_axis=0, concat_axis=0, tiled=True)
    tokens = tokens.reshape(-1, tokens.shape[-1])
    near, far = dot_pieces(tokens, pieces)
    segments = lambda qs: [q.reshape(n_y, -1, q.shape[1]) for q in qs]
    finish = lambda u: jax.nn.gelu(u, approximate=True).astype(jnp.bfloat16)
    return ring_reduce_scatter(segments(near), segments(far), "ry", n_y, finish)


def solution(mesh):
    n_row, n_col = mesh.shape["row"], mesh.shape["col"]
    nx = len({d.coords[0] for d in mesh.devices[:, 0]})
    split = Mesh(mesh.devices.reshape(n_row // nx, nx, n_col), ("ry", "rx", "col"))
    rows = ("ry", "rx")
    placed = (
        P(rows, "col"),
        P(rows, "col"),
        P(rows, "col"),
        P(rows, "col"),
        P(),
        P(rows, "col"),
    )

    def body(q_seq, k_seq, v_seq, resid, ln_gain, w_up):
        return per_device(q_seq, k_seq, v_seq, resid, ln_gain, w_up, nx)

    return jax.shard_map(body, mesh=split, in_specs=placed, out_specs=P(rows, "col"), check_vma=False)
```
